32 devices in a mesh: space: 8 (over z, x), fsdp: 4 (over y, core).
Axes of the slice: x: 2, y: 2, z: 4, core: 2. Of those that a mesh axis runs over, the one named last changes fastest.
Arguments:
- features: bfloat16 [4, 128, 8, 8, 512], P('fsdp', 'space'), may hold values from -6 to 6
- cotangent: bfloat16 [4, 128, 8, 8, 512], P('fsdp', 'space'), may hold values from -6 to 6
- tissue: int32 [4, 128], P('fsdp', 'space'), may hold values 0 or 1
- weight: bfloat16 [27, 64, 64], P(None, 'fsdp'), may hold values from -0.15625 to 0.15625
Outputs:
- activations: bfloat16 [4, 128, 8, 8, 512], P('fsdp', 'space')
- input_grad: bfloat16 [4, 128, 8, 8, 512], P('fsdp', 'space')
- weight_grad: float32 [27, 64, 64], P(None, 'fsdp')
The draws below stay inside these ranges and needn't reach their ends.
All inputs are finite; a program needn't handle non-finite values. No bound on the sum of `tissue` on one device may be relied on, other than what follows from the above.
Results may differ from the reference program's by a relative error of at most 0.0034.
Values may be sent and summed in bfloat16 or wider, within the bound.
No kernel may reach another device: no remote copies, remote signals or barrier semaphores. Data moves between devices by JAX's collectives and lax.ppermute only.
A program may use at most 192 MiB of HBM per device.

```python
import jax
import jax.numpy as jnp
from jax import lax

CHANNELS = 64
EDGE = 8
BRICK_X = 2
BRICK_Y = 2
BRICK_Z = 4
BRICKS = 128
SECTIONS = 4
N_SPACE = 8


def place_ends(values, rng, smallest, high):
    longest = values.shape.index(max(values.shape))
    spots = []
    for shift in (0, 1):
        where = [jax.random.randint(jax.random.fold_in(rng, axis), (), 0, length) for axis, length in enumerate(values.shape)]
        where[longest] = (where[longest] + shift) % values.shape[longest]
        spots.append(tuple(where))
    return values.at[spots[0]].set(smallest).at[spots[1]].set(high)


def block_levels(key, extent, pieces, smallest, largest):
    gain, own = 1.0, jax.random.fold_in(key, 6)
    for axis_at, blocks in pieces:
        draws = jnp.exp(jax.random.uniform(jax.random.fold_in(own, axis_at), (blocks,), jnp.float32, smallest / len(pieces), largest / len(pieces)))
        gain = gain * jnp.repeat(draws, extent[axis_at] // blocks).reshape([-1 if axis == axis_at else 1 for axis in range(len(extent))])
    return gain


def noise(stream_key, shape, spread, bound, cuts=(), kind=jnp.bfloat16):
    array = jax.random.normal(stream_key, shape, jnp.float32) * spread
    if len(cuts) > 0:
        array = block_levels(stream_key, shape, cuts, -0.22, 0.18) * array
    return jnp.clip(array, min=-bound, max=bound).astype(kind)


def setup_inputs(seed: int = 0) -> dict:
    keys = jax.random.split(jax.random.key(seed), 5)
    features = noise(keys[0], (SECTIONS, BRICKS, EDGE, EDGE, EDGE * CHANNELS), 1.0, 6.0, ((0, 4), (1, 8)))
    cotangent = noise(keys[1], (SECTIONS, BRICKS, EDGE, EDGE, EDGE * CHANNELS), 1.0, 6.0, ((0, 4), (1, 8)))
    tissue = place_ends((jax.random.randint(keys[2], (SECTIONS, BRICKS), 0, 4) < 3).astype(jnp.int32), jax.random.fold_in(keys[2], 1), 0, 1)
    weight = noise(keys[3], (27, CHANNELS, CHANNELS), (27 * CHANNELS) ** -0.5, 0.15625, ((1, 4),))
    return dict(features=features, cotangent=cotangent, tissue=tissue, weight=weight)


def grid_shape(number):
    factors = [1, 1, 1]
    places = 0
    while number % 2 == 0:
        factors[places % 3] = factors[places % 3] * 2
        number = number // 2
        places = places + 1
    factors[0] = factors[0] * number
    return factors

def to_section(bricks, grid_dims):
    blocks = bricks.reshape(grid_dims[0], grid_dims[1], grid_dims[2], BRICK_X, BRICK_Y, BRICK_Z, EDGE, EDGE, EDGE, CHANNELS)
    blocks = blocks.transpose(0, 3, 6, 1, 4, 7, 2, 5, 8, 9)
    return blocks.reshape(grid_dims[0] * BRICK_X * EDGE, grid_dims[1] * BRICK_Y * EDGE, grid_dims[2] * BRICK_Z * EDGE, CHANNELS)

def to_bricks(volume, grid_dims):
    blocks = volume.reshape(grid_dims[0], BRICK_X, EDGE, grid_dims[1], BRICK_Y, EDGE, grid_dims[2], BRICK_Z, EDGE, CHANNELS)
    blocks = blocks.transpose(0, 3, 6, 1, 4, 7, 2, 5, 8, 9)
    return blocks.reshape(BRICKS, EDGE, EDGE, EDGE * CHANNELS)

def convolve(volume, kernel):
    return lax.conv_general_dilated(volume[None], kernel, (1, 1, 1), 'SAME', dimension_numbers=('NDHWC', 'DHWIO', 'NDHWC'), precision=lax.Precision.HIGHEST)[0]

def reference(features, cotangent, tissue, weight):
    grid_dims = grid_shape(N_SPACE)
    kernel = weight.astype(jnp.float32).reshape(3, 3, 3, CHANNELS, CHANNELS)
    outs_act = []
    outs_grad = []
    grad_sum = jnp.zeros((3, 3, 3, CHANNELS, CHANNELS), jnp.float32)
    for section in range(SECTIONS):
        tissue_mask = jnp.broadcast_to(tissue[section].astype(jnp.float32)[:, None, None, None], features[section].shape)
        inputs = features[section].astype(jnp.float32)
        incoming = cotangent[section].astype(jnp.float32)
        masked = to_section(inputs * tissue_mask, grid_dims)
        pre_act, back_fn = jax.vjp(convolve, masked, kernel)
        pre_act = to_bricks(pre_act, grid_dims)
        gate_val = jax.nn.sigmoid(pre_act)
        outs_act.append((tissue_mask * (inputs + pre_act * gate_val)).astype(jnp.bfloat16))
        slope = gate_val * (1.0 + pre_act * (1.0 - gate_val))
        grad_pre = (tissue_mask * incoming * slope).astype(jnp.bfloat16).astype(jnp.float32)
        back_conv, kernel_grad = back_fn(to_section(grad_pre, grid_dims))
        back_conv = to_bricks(back_conv, grid_dims)
        outs_grad.append((tissue_mask * (incoming + back_conv)).astype(jnp.bfloat16))
        grad_sum = grad_sum + kernel_grad
    total_cells = SECTIONS * BRICKS * EDGE ** 3
    weight_grad = (grad_sum / jnp.sqrt(jnp.float32(total_cells))).reshape(27, CHANNELS, CHANNELS)
    return (jnp.stack(outs_act), jnp.stack(outs_grad), weight_grad)
```

```python
import math

import jax
import jax.numpy as jnp
from jax import lax
from jax.sharding import PartitionSpec as P

BRICK_X = 2
BRICK_Y = 2
BRICK_Z = 4
PAIR = 2
DEPTH = 2

CONV_DIMS = ("NDHWC", "DHWIO", "NDHWC")


def from_behind(shard, axis, by):
    peers = lax.axis_size(axis)
    pairs = [(i, i + by) for i in range(peers) if 0 <= i + by < peers]
    return lax.ppermute(shard, axis, pairs)


def grid_shape(number):
    factors = [1, 1, 1]
    places = 0
    while number % 2 == 0:
        factors[places % 3] = factors[places % 3] * 2
        number = number // 2
        places = places + 1
    factors[0] = factors[0] * number
    return factors


def to_volume(bricks, edge_cells, lanes):
    per_brick = edge_cells // PAIR
    blocks = bricks.reshape(
        BRICK_X, BRICK_Y, BRICK_Z, edge_cells, edge_cells, per_brick, lanes
    )
    blocks = blocks.transpose(0, 3, 1, 4, 2, 5, 6)
    return blocks.reshape(
        BRICK_X * edge_cells, BRICK_Y * edge_cells, BRICK_Z * per_brick, lanes
    )


def to_bricks(volume, edge_cells, lanes):
    per_brick = edge_cells // PAIR
    blocks = volume.reshape(
        BRICK_X, edge_cells, BRICK_Y, edge_cells, BRICK_Z, per_brick, lanes
    )
    blocks = blocks.transpose(0, 2, 4, 1, 3, 5, 6)
    return blocks.reshape(
        BRICK_X * BRICK_Y * BRICK_Z, edge_cells, edge_cells, per_brick * lanes
    )


def neighbour_plane(portion, offset, present):
    arrived = from_behind(portion, "space", offset)
    return jnp.where(present, arrived, jnp.zeros_like(arrived))


def extend(volume, grid_dims, places, widths):
    strides = (grid_dims[1] * grid_dims[2], grid_dims[2], 1)
    for axis_pos in range(3):
        axis = axis_pos + 1
        extent = volume.shape[axis]
        width = widths[axis_pos]
        last_layer = lax.slice_in_dim(volume, extent - width, extent, axis=axis)
        first_layer = lax.slice_in_dim(volume, 0, width, axis=axis)
        from_below = neighbour_plane(last_layer, strides[axis_pos], places[axis_pos] > 0)
        from_above = neighbour_plane(
            first_layer, -strides[axis_pos], places[axis_pos] < grid_dims[axis_pos] - 1
        )
        volume = jnp.concatenate([from_below, volume, from_above], axis=axis)
    return volume


def super_kernel(weight_full, channels):
    taps = weight_full.reshape(3, 3, 3, channels, channels)
    zero = jnp.zeros((3, 3, channels, channels), weight_full.dtype)
    rows = []
    for dz in range(3):
        row = []
        for hi in range(PAIR):
            col = []
            for ho in range(PAIR):
                c = 2 * dz - 1 + hi - ho
                col.append(taps[:, :, c] if 0 <= c < 3 else zero)
            row.append(jnp.concatenate(col, axis=-1))
        rows.append(jnp.concatenate(row, axis=-2))
    return jnp.stack(rows, axis=2)


def fold_kernel_grad(grad_sup, channels):
    taps = [None, None, None]
    for dz in range(3):
        for hi in range(PAIR):
            for ho in range(PAIR):
                c = 2 * dz - 1 + hi - ho
                if 0 <= c < 3:
                    block = grad_sup[
                        :, :, dz, hi * channels : (hi + 1) * channels, ho * channels : (ho + 1) * channels
                    ]
                    taps[c] = block if taps[c] is None else taps[c] + block
    return jnp.stack(taps, axis=2).reshape(27, channels, channels)


def conv(volume, kernel):
    return lax.conv_general_dilated(
        volume[None],
        kernel,
        (1, 1, 1),
        "VALID",
        dimension_numbers=CONV_DIMS,
        preferred_element_type=jnp.float32,
    )[0]


def kernel_grad(inputs, grads):
    out = lax.conv_general_dilated(
        inputs[None],
        grads[None],
        (1, 1, 1),
        "VALID",
        dimension_numbers=("CDHWN", "IDHWO", "NDHWC"),
        preferred_element_type=jnp.float32,
    )
    return out.transpose(1, 2, 3, 0, 4)


def local(features, cotangent, tissue, weight):
    edge_cells = features.shape[2]
    channels = weight.shape[2]
    lanes = PAIR * channels
    grid_dims = grid_shape(lax.axis_size("space"))
    index_now = lax.axis_index("space")
    places = (
        index_now // (grid_dims[1] * grid_dims[2]),
        index_now // grid_dims[2] % grid_dims[1],
        index_now % grid_dims[2],
    )
    weight_full = lax.all_gather(weight, "fsdp", axis=1, tiled=True)
    k_fwd = super_kernel(weight_full, channels)
    k_back = jnp.flip(k_fwd, (0, 1, 2)).transpose(0, 1, 2, 4, 3)

    present = tissue[0][:, None, None, None] > 0
    inputs = features[0]
    incoming = cotangent[0]
    masked = jnp.where(present, inputs, jnp.zeros_like(inputs))
    masked_cot = jnp.where(present, incoming, jnp.zeros_like(incoming))

    both = jnp.stack(
        [to_volume(masked, edge_cells, lanes), to_volume(masked_cot, edge_cells, lanes)]
    )
    grown = extend(both, grid_dims, places, (DEPTH, DEPTH, 1))
    grown = jnp.pad(grown, ((0, 0), (0, 0), (0, 0), (1, 1), (0, 0)))
    padded_in = grown[0]
    cot_ext = grown[1, 1:-1, 1:-1, 1:-1]

    pre_ext = conv(padded_in, k_fwd)
    gate_ext = jax.nn.sigmoid(pre_ext)
    slope_ext = gate_ext * (1.0 + pre_ext * (1.0 - gate_ext))
    grad_ext = (cot_ext.astype(jnp.float32) * slope_ext).astype(jnp.bfloat16)

    tissue_mask = tissue[0].astype(jnp.float32)[:, None, None, None]
    pre = to_bricks(pre_ext[1:-1, 1:-1, 1:-1], edge_cells, lanes)
    gate_val = to_bricks(gate_ext[1:-1, 1:-1, 1:-1], edge_cells, lanes)
    activations = (tissue_mask * (inputs.astype(jnp.float32) + pre * gate_val)).astype(
        jnp.bfloat16
    )

    back = to_bricks(conv(grad_ext, k_back), edge_cells, lanes)
    input_grad = (tissue_mask * (incoming.astype(jnp.float32) + back)).astype(jnp.bfloat16)

    total_cells = (
        lax.axis_size("space") * lax.axis_size("fsdp") * BRICK_X * BRICK_Y * BRICK_Z * edge_cells**3
    )
    grad_sup = kernel_grad(padded_in[1:-1, 1:-1, 1:-1], grad_ext[1:-1, 1:-1, 1:-1])
    grad_term = fold_kernel_grad(grad_sup, channels) / math.sqrt(total_cells)
    grad_part = lax.psum_scatter(grad_term, "fsdp", scatter_dimension=1, tiled=True)
    grad_part = lax.psum(grad_part, "space")
    return (activations[None], input_grad[None], grad_part)


def solution(mesh):
    return jax.shard_map(
        local,
        mesh=mesh,
        in_specs=(
            P("fsdp", "space", None, None, None),
            P("fsdp", "space", None, None, None),
            P("fsdp", "space"),
            P(None, "fsdp", None),
        ),
        out_specs=(
            P("fsdp", "space", None, None, None),
            P("fsdp", "space", None, None, None),
            P(None, "fsdp", None),
        ),
        check_vma=False,
    )
```

```python
import math

import jax
import jax.numpy as jnp
from jax import lax
from jax.sharding import PartitionSpec as P

BRICK_X = 2
BRICK_Y = 2
BRICK_Z = 4
PAIR = 2
DEPTH = 2

CONV_DIMS = ("NDHWC", "DHWIO", "NDHWC")


def from_behind(shard, axis, by):
    peers = lax.axis_size(axis)
    pairs = [(i, i + by) for i in range(peers) if 0 <= i + by < peers]
    return lax.ppermute(shard, axis, pairs)


def grid_shape(number):
    factors = [1, 1, 1]
    places = 0
    while number % 2 == 0:
        factors[places % 3] = factors[places % 3] * 2
        number = number // 2
        places = places + 1
    factors[0] = factors[0] * number
    return factors


def to_volume(bricks, edge_cells, lanes):
    per_brick = edge_cells // PAIR
    blocks = bricks.reshape(
        BRICK_X, BRICK_Y, BRICK_Z, edge_cells, edge_cells, per_brick, lanes
    )
    blocks = blocks.transpose(0, 3, 1, 4, 2, 5, 6)
    return blocks.reshape(
        BRICK_X * edge_cells, BRICK_Y * edge_cells, BRICK_Z * per_brick, lanes
    )


def to_bricks(volume, edge_cells, lanes):
    per_brick = edge_cells // PAIR
    blocks = volume.reshape(
        BRICK_X, edge_cells, BRICK_Y, edge_cells, BRICK_Z, per_brick, lanes
    )
    blocks = blocks.transpose(0, 2, 4, 1, 3, 5, 6)
    return blocks.reshape(
        BRICK_X * BRICK_Y * BRICK_Z, edge_cells, edge_cells, per_brick * lanes
    )


def neighbour_plane(portion, offset, present):
    arrived = from_behind(portion, "space", offset)
    return jnp.where(present, arrived, jnp.zeros_like(arrived))


def extend(volume, grid_dims, places, widths):
    strides = (grid_dims[1] * grid_dims[2], grid_dims[2], 1)
    for axis_pos in range(3):
        axis = axis_pos + 1
        extent = volume.shape[axis]
        width = widths[axis_pos]
        last_layer = lax.slice_in_dim(volume, extent - width, extent, axis=axis)
        first_layer = lax.slice_in_dim(volume, 0, width, axis=axis)
        from_below = neighbour_plane(last_layer, strides[axis_pos], places[axis_pos] > 0)
        from_above = neighbour_plane(
            first_layer, -strides[axis_pos], places[axis_pos] < grid_dims[axis_pos] - 1
        )
        volume = jnp.concatenate([from_below, volume, from_above], axis=axis)
    return volume


def super_kernel(weight_full, channels):
    taps = weight_full.reshape(3, 3, 3, channels, channels)
    zero = jnp.zeros((3, 3, channels, channels), weight_full.dtype)
    rows = []
    for dz in range(3):
        row = []
        for hi in range(PAIR):
            col = []
            for ho in range(PAIR):
                c = 2 * dz - 1 + hi - ho
                col.append(taps[:, :, c] if 0 <= c < 3 else zero)
            row.append(jnp.concatenate(col, axis=-1))
        rows.append(jnp.concatenate(row, axis=-2))
    return jnp.stack(rows, axis=2)


def fold_kernel_grad(grad_sup, channels):
    taps = [None, None, None]
    for dz in range(3):
        for hi in range(PAIR):
            for ho in range(PAIR):
                c = 2 * dz - 1 + hi - ho
                if 0 <= c < 3:
                    block = grad_sup[
                        :, :, dz, hi * channels : (hi + 1) * channels, ho * channels : (ho + 1) * channels
                    ]
                    taps[c] = block if taps[c] is None else taps[c] + block
    return jnp.stack(taps, axis=2).reshape(27, channels, channels)


def conv(volume, kernel):
    return lax.conv_general_dilated(
        volume[None],
        kernel,
        (1, 1, 1),
        "VALID",
        dimension_numbers=CONV_DIMS,
        preferred_element_type=jnp.float32,
    )[0]


def kernel_grad(inputs, grads):
    out = lax.conv_general_dilated(
        inputs[None],
        grads[None],
        (1, 1, 1),
        "VALID",
        dimension_numbers=("CDHWN", "IDHWO", "NDHWC"),
        preferred_element_type=jnp.float32,
    )
    return out.transpose(1, 2, 3, 0, 4)


def exchange(value, axis, distance):
    peers = lax.axis_size(axis)
    return lax.ppermute(value, axis, [(i, i ^ distance) for i in range(peers)])


def reduce_scatter_fsdp(term):
    peers = lax.axis_size("fsdp")
    if peers & (peers - 1):
        return lax.psum_scatter(term, "fsdp", scatter_dimension=1, tiled=True)
    index = lax.axis_index("fsdp")
    distance = peers // 2
    while distance >= 1:
        half = term.shape[1] // 2
        keep = (index // distance) % 2
        mine = lax.dynamic_slice_in_dim(term, keep * half, half, 1)
        theirs = lax.dynamic_slice_in_dim(term, (1 - keep) * half, half, 1)
        term = mine + exchange(theirs, "fsdp", distance)
        distance //= 2
    return term


def all_reduce_space(term):
    peers = lax.axis_size("space")
    if peers & (peers - 1):
        return lax.psum(term, "space")
    distance = 1
    while distance < peers:
        term = term + exchange(term, "space", distance)
        distance *= 2
    return term


def local(features, cotangent, tissue, weight):
    edge_cells = features.shape[2]
    channels = weight.shape[2]
    lanes = PAIR * channels
    grid_dims = grid_shape(lax.axis_size("space"))
    index_now = lax.axis_index("space")
    places = (
        index_now // (grid_dims[1] * grid_dims[2]),
        index_now // grid_dims[2] % grid_dims[1],
        index_now % grid_dims[2],
    )
    weight_full = lax.all_gather(weight, "fsdp", axis=1, tiled=True)
    k_fwd = super_kernel(weight_full, channels)
    k_back = jnp.flip(k_fwd, (0, 1, 2)).transpose(0, 1, 2, 4, 3)

    present = tissue[0][:, None, None, None] > 0
    inputs = features[0]
    incoming = cotangent[0]
    masked = jnp.where(present, inputs, jnp.zeros_like(inputs))
    masked_cot = jnp.where(present, incoming, jnp.zeros_like(incoming))

    both = jnp.stack(
        [to_volume(masked, edge_cells, lanes), to_volume(masked_cot, edge_cells, lanes)]
    )
    grown = extend(both, grid_dims, places, (DEPTH, DEPTH, 1))
    grown = jnp.pad(grown, ((0, 0), (0, 0), (0, 0), (1, 1), (0, 0)))
    padded_in = grown[0]
    cot_ext = grown[1, 1:-1, 1:-1, 1:-1]

    pre_ext = conv(padded_in, k_fwd)
    gate_ext = jax.nn.sigmoid(pre_ext)
    slope_ext = gate_ext * (1.0 + pre_ext * (1.0 - gate_ext))
    grad_ext = (cot_ext.astype(jnp.float32) * slope_ext).astype(jnp.bfloat16)

    tissue_mask = tissue[0].astype(jnp.float32)[:, None, None, None]
    pre = to_bricks(pre_ext[1:-1, 1:-1, 1:-1], edge_cells, lanes)
    gate_val = to_bricks(gate_ext[1:-1, 1:-1, 1:-1], edge_cells, lanes)
    activations = (tissue_mask * (inputs.astype(jnp.float32) + pre * gate_val)).astype(
        jnp.bfloat16
    )

    back = to_bricks(conv(grad_ext, k_back), edge_cells, lanes)
    input_grad = (tissue_mask * (incoming.astype(jnp.float32) + back)).astype(jnp.bfloat16)

    total_cells = (
        lax.axis_size("space") * lax.axis_size("fsdp") * BRICK_X * BRICK_Y * BRICK_Z * edge_cells**3
    )
    grad_sup = kernel_grad(padded_in[1:-1, 1:-1, 1:-1], grad_ext[1:-1, 1:-1, 1:-1])
    grad_term = fold_kernel_grad(grad_sup, channels) / math.sqrt(total_cells)
    grad_part = reduce_scatter_fsdp(grad_term)
    grad_part = all_reduce_space(grad_part)
    return (activations[None], input_grad[None], grad_part)


def solution(mesh):
    return jax.shard_map(
        local,
        mesh=mesh,
        in_specs=(
            P("fsdp", "space", None, None, None),
            P("fsdp", "space", None, None, None),
            P("fsdp", "space"),
            P(None, "fsdp", None),
        ),
        out_specs=(
            P("fsdp", "space", None, None, None),
            P("fsdp", "space", None, None, None),
            P(None, "fsdp", None),
        ),
        check_vma=False,
    )
```

```python
import math

import jax
import jax.numpy as jnp
from jax import lax
from jax.sharding import PartitionSpec as P

BRICK_X = 2
BRICK_Y = 2
BRICK_Z = 4
PAIR = 2
DEPTH = 2

CONV_DIMS = ("NDHWC", "DHWIO", "NDHWC")


def from_behind(shard, axis, by):
    peers = lax.axis_size(axis)
    pairs = [(i, i + by) for i in range(peers) if 0 <= i + by < peers]
    return lax.ppermute(shard, axis, pairs)


def grid_shape(number):
    factors = [1, 1, 1]
    places = 0
    while number % 2 == 0:
        factors[places % 3] = factors[places % 3] * 2
        number = number // 2
        places = places + 1
    factors[0] = factors[0] * number
    return factors


def to_volume(bricks, edge_cells, lanes):
    per_brick = edge_cells // PAIR
    blocks = bricks.reshape(
        BRICK_X, BRICK_Y, BRICK_Z, edge_cells, edge_cells, per_brick, lanes
    )
    blocks = blocks.transpose(0, 3, 1, 4, 2, 5, 6)
    return blocks.reshape(
        BRICK_X * edge_cells, BRICK_Y * edge_cells, BRICK_Z * per_brick, lanes
    )


def to_bricks(volume, edge_cells, lanes):
    per_brick = edge_cells // PAIR
    blocks = volume.reshape(
        BRICK_X, edge_cells, BRICK_Y, edge_cells, BRICK_Z, per_brick, lanes
    )
    blocks = blocks.transpose(0, 2, 4, 1, 3, 5, 6)
    return blocks.reshape(
        BRICK_X * BRICK_Y * BRICK_Z, edge_cells, edge_cells, per_brick * lanes
    )


def neighbour_plane(portion, offset, present):
    arrived = from_behind(portion, "space", offset)
    return jnp.where(present, arrived, jnp.zeros_like(arrived))


def extend(volume, grid_dims, places, widths):
    strides = (grid_dims[1] * grid_dims[2], grid_dims[2], 1)
    for axis_pos in range(3):
        axis = axis_pos + 1
        extent = volume.shape[axis]
        width = widths[axis_pos]
        last_layer = lax.slice_in_dim(volume, extent - width, extent, axis=axis)
        first_layer = lax.slice_in_dim(volume, 0, width, axis=axis)
        from_below = neighbour_plane(last_layer, strides[axis_pos], places[axis_pos] > 0)
        from_above = neighbour_plane(
            first_layer, -strides[axis_pos], places[axis_pos] < grid_dims[axis_pos] - 1
        )
        volume = jnp.concatenate([from_below, volume, from_above], axis=axis)
    return volume


def super_kernel(weight_full, channels):
    taps = weight_full.reshape(3, 3, 3, channels, channels)
    zero = jnp.zeros((3, 3, channels, channels), weight_full.dtype)
    rows = []
    for dz in range(3):
        row = []
        for hi in range(PAIR):
            col = []
            for ho in range(PAIR):
                c = 2 * dz - 1 + hi - ho
                col.append(taps[:, :, c] if 0 <= c < 3 else zero)
            row.append(jnp.concatenate(col, axis=-1))
        rows.append(jnp.concatenate(row, axis=-2))
    return jnp.stack(rows, axis=2)


def fold_kernel_grad(grad_sup, channels):
    taps = [None, None, None]
    for dz in range(3):
        for hi in range(PAIR):
            for ho in range(PAIR):
                c = 2 * dz - 1 + hi - ho
                if 0 <= c < 3:
                    block = grad_sup[
                        :, :, dz, hi * channels : (hi + 1) * channels, ho * channels : (ho + 1) * channels
                    ]
                    taps[c] = block if taps[c] is None else taps[c] + block
    return jnp.stack(taps, axis=2).reshape(27, channels, channels)


def conv(volume, kernel):
    return lax.conv_general_dilated(
        volume[None],
        kernel,
        (1, 1, 1),
        "VALID",
        dimension_numbers=CONV_DIMS,
        preferred_element_type=jnp.float32,
    )[0]


def kernel_grad(inputs, grads):
    size_x, size_y, size_s, lanes = grads.shape
    shifted = jnp.concatenate([inputs[:, :, dz : dz + size_s] for dz in range(3)], axis=-1)
    rows = grads.reshape(size_x * size_y * size_s, lanes)
    pieces = []
    for a in range(3):
        for b in range(3):
            window = shifted[a : a + size_x, b : b + size_y].reshape(
                size_x * size_y * size_s, 3 * lanes
            )
            pieces.append(
                lax.dot_general(
                    window, rows, (((0,), (0,)), ((), ())), preferred_element_type=jnp.float32
                )
            )
    return jnp.stack(pieces).reshape(3, 3, 3, lanes, lanes)


def exchange(value, axis, distance):
    peers = lax.axis_size(axis)
    return lax.ppermute(value, axis, [(i, i ^ distance) for i in range(peers)])


def reduce_scatter_fsdp(term):
    peers = lax.axis_size("fsdp")
    if peers & (peers - 1):
        return lax.psum_scatter(term, "fsdp", scatter_dimension=1, tiled=True)
    index = lax.axis_index("fsdp")
    distance = peers // 2
    while distance >= 1:
        half = term.shape[1] // 2
        keep = (index // distance) % 2
        mine = lax.dynamic_slice_in_dim(term, keep * half, half, 1)
        theirs = lax.dynamic_slice_in_dim(term, (1 - keep) * half, half, 1)
        term = mine + exchange(theirs, "fsdp", distance)
        distance //= 2
    return term


def all_reduce_space(term):
    peers = lax.axis_size("space")
    if peers & (peers - 1):
        return lax.psum(term, "space")
    distance = 1
    while distance < peers:
        term = term + exchange(term, "space", distance)
        distance *= 2
    return term


def local(features, cotangent, tissue, weight):
    edge_cells = features.shape[2]
    channels = weight.shape[2]
    lanes = PAIR * channels
    grid_dims = grid_shape(lax.axis_size("space"))
    index_now = lax.axis_index("space")
    places = (
        index_now // (grid_dims[1] * grid_dims[2]),
        index_now // grid_dims[2] % grid_dims[1],
        index_now % grid_dims[2],
    )
    weight_full = lax.all_gather(weight, "fsdp", axis=1, tiled=True)
    k_fwd = super_kernel(weight_full, channels)
    k_back = jnp.flip(k_fwd, (0, 1, 2)).transpose(0, 1, 2, 4, 3)

    present = tissue[0][:, None, None, None] > 0
    inputs = features[0]
    incoming = cotangent[0]
    masked = jnp.where(present, inputs, jnp.zeros_like(inputs))
    masked_cot = jnp.where(present, incoming, jnp.zeros_like(incoming))

    both = jnp.stack(
        [to_volume(masked, edge_cells, lanes), to_volume(masked_cot, edge_cells, lanes)]
    )
    grown = extend(both, grid_dims, places, (DEPTH, DEPTH, 1))
    grown = jnp.pad(grown, ((0, 0), (0, 0), (0, 0), (1, 1), (0, 0)))
    padded_in = grown[0]
    cot_ext = grown[1, 1:-1, 1:-1, 1:-1]

    pre_ext = conv(padded_in, k_fwd)
    gate_ext = jax.nn.sigmoid(pre_ext)
    slope_ext = gate_ext * (1.0 + pre_ext * (1.0 - gate_ext))
    grad_ext = (cot_ext.astype(jnp.float32) * slope_ext).astype(jnp.bfloat16)

    tissue_mask = tissue[0].astype(jnp.float32)[:, None, None, None]
    pre = to_bricks(pre_ext[1:-1, 1:-1, 1:-1], edge_cells, lanes)
    gate_val = to_bricks(gate_ext[1:-1, 1:-1, 1:-1], edge_cells, lanes)
    activations = (tissue_mask * (inputs.astype(jnp.float32) + pre * gate_val)).astype(
        jnp.bfloat16
    )

    back = to_bricks(conv(grad_ext, k_back), edge_cells, lanes)
    input_grad = (tissue_mask * (incoming.astype(jnp.float32) + back)).astype(jnp.bfloat16)

    total_cells = (
        lax.axis_size("space") * lax.axis_size("fsdp") * BRICK_X * BRICK_Y * BRICK_Z * edge_cells**3
    )
    grad_sup = kernel_grad(padded_in[1:-1, 1:-1, 1:-1], grad_ext[1:-1, 1:-1, 1:-1])
    grad_term = fold_kernel_grad(grad_sup, channels) / math.sqrt(total_cells)
    grad_part = reduce_scatter_fsdp(grad_term)
    grad_part = all_reduce_space(grad_part)
    return (activations[None], input_grad[None], grad_part)


def solution(mesh):
    return jax.shard_map(
        local,
        mesh=mesh,
        in_specs=(
            P("fsdp", "space", None, None, None),
            P("fsdp", "space", None, None, None),
            P("fsdp", "space"),
            P(None, "fsdp", None),
        ),
        out_specs=(
            P("fsdp", "space", None, None, None),
            P("fsdp", "space", None, None, None),
            P(None, "fsdp", None),
        ),
        check_vma=False,
    )
```

```python
import math

import jax
import jax.numpy as jnp
from jax import lax
from jax.sharding import PartitionSpec as P

BRICK_X = 2
BRICK_Y = 2
BRICK_Z = 4
PAIR = 2
DEPTH = 2

CONV_DIMS = ("NDHWC", "DHWIO", "NDHWC")


def from_behind(shard, axis, by):
    peers = lax.axis_size(axis)
    pairs = [(i, i + by) for i in range(peers) if 0 <= i + by < peers]
    return lax.ppermute(shard, axis, pairs)


def grid_shape(number):
    factors = [1, 1, 1]
    places = 0
    while number % 2 == 0:
        factors[places % 3] = factors[places % 3] * 2
        number = number // 2
        places = places + 1
    factors[0] = factors[0] * number
    return factors


def to_volume(bricks, edge_cells, lanes):
    per_brick = edge_cells // PAIR
    blocks = bricks.reshape(
        BRICK_X, BRICK_Y, BRICK_Z, edge_cells, edge_cells, per_brick, lanes
    )
    blocks = blocks.transpose(0, 3, 1, 4, 2, 5, 6)
    return blocks.reshape(
        BRICK_X * edge_cells, BRICK_Y * edge_cells, BRICK_Z * per_brick, lanes
    )


def to_bricks(volume, edge_cells, lanes):
    per_brick = edge_cells // PAIR
    blocks = volume.reshape(
        BRICK_X, edge_cells, BRICK_Y, edge_cells, BRICK_Z, per_brick, lanes
    )
    blocks = blocks.transpose(0, 2, 4, 1, 3, 5, 6)
    return blocks.reshape(
        BRICK_X * BRICK_Y * BRICK_Z, edge_cells, edge_cells, per_brick * lanes
    )


def neighbour_plane(portion, offset, present):
    arrived = from_behind(portion, "space", offset)
    return jnp.where(present, arrived, jnp.zeros_like(arrived))


def extend(volume, grid_dims, places, widths):
    strides = (grid_dims[1] * grid_dims[2], grid_dims[2], 1)
    for axis_pos in range(3):
        axis = axis_pos + 1
        extent = volume.shape[axis]
        width = widths[axis_pos]
        last_layer = lax.slice_in_dim(volume, extent - width, extent, axis=axis)
        first_layer = lax.slice_in_dim(volume, 0, width, axis=axis)
        from_below = neighbour_plane(last_layer, strides[axis_pos], places[axis_pos] > 0)
        from_above = neighbour_plane(
            first_layer, -strides[axis_pos], places[axis_pos] < grid_dims[axis_pos] - 1
        )
        volume = jnp.concatenate([from_below, volume, from_above], axis=axis)
    return volume


def super_kernel(weight_full, channels):
    taps = weight_full.reshape(3, 3, 3, channels, channels)
    zero = jnp.zeros((3, 3, channels, channels), weight_full.dtype)
    rows = []
    for dz in range(3):
        row = []
        for hi in range(PAIR):
            col = []
            for ho in range(PAIR):
                c = 2 * dz - 1 + hi - ho
                col.append(taps[:, :, c] if 0 <= c < 3 else zero)
            row.append(jnp.concatenate(col, axis=-1))
        rows.append(jnp.concatenate(row, axis=-2))
    return jnp.stack(rows, axis=2)


def fold_kernel_grad(grad_sup, channels):
    taps = [None, None, None]
    for dz in range(3):
        for hi in range(PAIR):
            for ho in range(PAIR):
                c = 2 * dz - 1 + hi - ho
                if 0 <= c < 3:
                    block = grad_sup[
                        :, :, dz, hi * channels : (hi + 1) * channels, ho * channels : (ho + 1) * channels
                    ]
                    taps[c] = block if taps[c] is None else taps[c] + block
    return jnp.stack(taps, axis=2).reshape(27, channels, channels)


def conv(volume, kernel):
    return lax.conv_general_dilated(
        volume[None],
        kernel,
        (1, 1, 1),
        "VALID",
        dimension_numbers=CONV_DIMS,
        preferred_element_type=jnp.float32,
    )[0]


def kernel_grad(inputs, grads):
    size_x, size_y, size_s, lanes = grads.shape
    shifted = jnp.concatenate([inputs[:, :, dz : dz + size_s] for dz in range(3)], axis=-1)
    rows = grads.reshape(size_x * size_y * size_s, lanes)
    pieces = []
    for a in range(3):
        for b in range(3):
            window = shifted[a : a + size_x, b : b + size_y].reshape(
                size_x * size_y * size_s, 3 * lanes
            )
            pieces.append(
                lax.dot_general(
                    window, rows, (((0,), (0,)), ((), ())), preferred_element_type=jnp.float32
                )
            )
    return jnp.stack(pieces).reshape(3, 3, 3, lanes, lanes)


def exchange(value, axis, distance):
    peers = lax.axis_size(axis)
    return lax.ppermute(value, axis, [(i, i ^ distance) for i in range(peers)])


def pairwise_sum(values):
    while len(values) > 1:
        values = [values[m] + values[m + 1] for m in range(0, len(values), 2)]
    return values[0]


def reduce_scatter_fsdp(term):
    peers = lax.axis_size("fsdp")
    if peers & (peers - 1):
        return lax.psum_scatter(term, "fsdp", scatter_dimension=1, tiled=True)
    index = lax.axis_index("fsdp")
    rows_each = term.shape[1] // peers
    received = [lax.dynamic_slice_in_dim(term, index * rows_each, rows_each, 1)]
    for k in range(1, peers):
        piece = lax.dynamic_slice_in_dim(term, (index ^ k) * rows_each, rows_each, 1)
        received.append(exchange(piece, "fsdp", k))
    return pairwise_sum(received)


def all_reduce_space(term, radix=8):
    peers = lax.axis_size("space")
    if peers & (peers - 1):
        return lax.psum(term, "space")
    distance = 1
    while distance < peers:
        group = min(radix, peers // distance)
        received = [term] + [exchange(term, "space", k * distance) for k in range(1, group)]
        term = pairwise_sum(received)
        distance *= group
    return term


def local(features, cotangent, tissue, weight):
    edge_cells = features.shape[2]
    channels = weight.shape[2]
    lanes = PAIR * channels
    grid_dims = grid_shape(lax.axis_size("space"))
    index_now = lax.axis_index("space")
    places = (
        index_now // (grid_dims[1] * grid_dims[2]),
        index_now // grid_dims[2] % grid_dims[1],
        index_now % grid_dims[2],
    )
    weight_full = lax.all_gather(weight, "fsdp", axis=1, tiled=True)
    k_fwd = super_kernel(weight_full, channels)
    k_back = jnp.flip(k_fwd, (0, 1, 2)).transpose(0, 1, 2, 4, 3)

    present = tissue[0][:, None, None, None] > 0
    inputs = features[0]
    incoming = cotangent[0]
    masked = jnp.where(present, inputs, jnp.zeros_like(inputs))
    masked_cot = jnp.where(present, incoming, jnp.zeros_like(incoming))

    both = jnp.stack(
        [to_volume(masked, edge_cells, lanes), to_volume(masked_cot, edge_cells, lanes)]
    )
    grown = extend(both, grid_dims, places, (DEPTH, DEPTH, 1))
    grown = jnp.pad(grown, ((0, 0), (0, 0), (0, 0), (1, 1), (0, 0)))
    padded_in = grown[0]
    cot_ext = grown[1, 1:-1, 1:-1, 1:-1]

    pre_ext = conv(padded_in, k_fwd)
    gate_ext = jax.nn.sigmoid(pre_ext)
    slope_ext = gate_ext * (1.0 + pre_ext * (1.0 - gate_ext))
    grad_ext = (cot_ext.astype(jnp.float32) * slope_ext).astype(jnp.bfloat16)

    tissue_mask = tissue[0].astype(jnp.float32)[:, None, None, None]
    pre = to_bricks(pre_ext[1:-1, 1:-1, 1:-1], edge_cells, lanes)
    gate_val = to_bricks(gate_ext[1:-1, 1:-1, 1:-1], edge_cells, lanes)
    activations = (tissue_mask * (inputs.astype(jnp.float32) + pre * gate_val)).astype(
        jnp.bfloat16
    )

    back = to_bricks(conv(grad_ext, k_back), edge_cells, lanes)
    input_grad = (tissue_mask * (incoming.astype(jnp.float32) + back)).astype(jnp.bfloat16)

    total_cells = (
        lax.axis_size("space") * lax.axis_size("fsdp") * BRICK_X * BRICK_Y * BRICK_Z * edge_cells**3
    )
    grad_sup = kernel_grad(padded_in[1:-1, 1:-1, 1:-1], grad_ext[1:-1, 1:-1, 1:-1])
    grad_term = fold_kernel_grad(grad_sup, channels) / math.sqrt(total_cells)
    grad_part = reduce_scatter_fsdp(grad_term)
    grad_part = all_reduce_space(grad_part)
    return (activations[None], input_grad[None], grad_part)


def solution(mesh):
    return jax.shard_map(
        local,
        mesh=mesh,
        in_specs=(
            P("fsdp", "space", None, None, None),
            P("fsdp", "space", None, None, None),
            P("fsdp", "space"),
            P(None, "fsdp", None),
        ),
        out_specs=(
            P("fsdp", "space", None, None, None),
            P("fsdp", "space", None, None, None),
            P(None, "fsdp", None),
        ),
        check_vma=False,
    )
```

```python
import math

import jax
import jax.numpy as jnp
from jax import lax
from jax.sharding import PartitionSpec as P

BRICK_X = 2
BRICK_Y = 2
BRICK_Z = 4
PAIR = 2
DEPTH = 2

def from_behind(shard, axis, by):
    peers = lax.axis_size(axis)
    pairs = [(i, i + by) for i in range(peers) if 0 <= i + by < peers]
    return lax.ppermute(shard, axis, pairs)


def grid_shape(number):
    factors = [1, 1, 1]
    places = 0
    while number % 2 == 0:
        factors[places % 3] = factors[places % 3] * 2
        number = number // 2
        places = places + 1
    factors[0] = factors[0] * number
    return factors


def to_volume(bricks, edge_cells, lanes):
    per_brick = edge_cells // PAIR
    blocks = bricks.reshape(
        BRICK_X, BRICK_Y, BRICK_Z, edge_cells, edge_cells, per_brick, lanes
    )
    blocks = blocks.transpose(0, 3, 1, 4, 2, 5, 6)
    return blocks.reshape(
        BRICK_X * edge_cells, BRICK_Y * edge_cells, BRICK_Z * per_brick, lanes
    )


def to_bricks(volume, edge_cells, lanes):
    per_brick = edge_cells // PAIR
    blocks = volume.reshape(
        BRICK_X, edge_cells, BRICK_Y, edge_cells, BRICK_Z, per_brick, lanes
    )
    blocks = blocks.transpose(0, 2, 4, 1, 3, 5, 6)
    return blocks.reshape(
        BRICK_X * BRICK_Y * BRICK_Z, edge_cells, edge_cells, per_brick * lanes
    )


def neighbour_plane(portion, offset, present):
    arrived = from_behind(portion, "space", offset)
    return jnp.where(present, arrived, jnp.zeros_like(arrived))


def extend(volume, grid_dims, places, widths):
    strides = (grid_dims[1] * grid_dims[2], grid_dims[2], 1)
    for axis_pos in range(3):
        axis = axis_pos + 1
        extent = volume.shape[axis]
        width = widths[axis_pos]
        last_layer = lax.slice_in_dim(volume, extent - width, extent, axis=axis)
        first_layer = lax.slice_in_dim(volume, 0, width, axis=axis)
        from_below = neighbour_plane(last_layer, strides[axis_pos], places[axis_pos] > 0)
        from_above = neighbour_plane(
            first_layer, -strides[axis_pos], places[axis_pos] < grid_dims[axis_pos] - 1
        )
        volume = jnp.concatenate([from_below, volume, from_above], axis=axis)
    return volume


def super_kernel(weight_full, channels):
    taps = weight_full.reshape(3, 3, 3, channels, channels)
    zero = jnp.zeros((3, 3, channels, channels), weight_full.dtype)
    rows = []
    for dz in range(3):
        row = []
        for hi in range(PAIR):
            col = []
            for ho in range(PAIR):
                c = 2 * dz - 1 + hi - ho
                col.append(taps[:, :, c] if 0 <= c < 3 else zero)
            row.append(jnp.concatenate(col, axis=-1))
        rows.append(jnp.concatenate(row, axis=-2))
    return jnp.stack(rows, axis=2)


def fold_kernel_grad(grad_sup, channels):
    taps = [None, None, None]
    for dz in range(3):
        for hi in range(PAIR):
            for ho in range(PAIR):
                c = 2 * dz - 1 + hi - ho
                if 0 <= c < 3:
                    block = grad_sup[
                        :, :, dz, hi * channels : (hi + 1) * channels, ho * channels : (ho + 1) * channels
                    ]
                    taps[c] = block if taps[c] is None else taps[c] + block
    return jnp.stack(taps, axis=2).reshape(27, channels, channels)


def z_shift(volume, start, count):
    return jnp.concatenate(
        [volume[:, :, start + dz : start + dz + count] for dz in range(3)], axis=-1
    )


def tap_dots(shifted, kernel, size_x, size_y):
    total = None
    for a in range(3):
        for b in range(3):
            term = lax.dot_general(
                shifted[a : a + size_x, b : b + size_y],
                kernel[a, b],
                (((3,), (0,)), ((), ())),
                preferred_element_type=jnp.float32,
            )
            total = term if total is None else total + term
    return total


def kernel_grad(inputs, grads):
    size_x, size_y, size_s, lanes = grads.shape
    shifted = jnp.concatenate([inputs[:, :, dz : dz + size_s] for dz in range(3)], axis=-1)
    rows = grads.reshape(size_x * size_y * size_s, lanes)
    pieces = []
    for a in range(3):
        for b in range(3):
            window = shifted[a : a + size_x, b : b + size_y].reshape(
                size_x * size_y * size_s, 3 * lanes
            )
            pieces.append(
                lax.dot_general(
                    window, rows, (((0,), (0,)), ((), ())), preferred_element_type=jnp.float32
                )
            )
    return jnp.stack(pieces).reshape(3, 3, 3, lanes, lanes)


def exchange(value, axis, distance):
    peers = lax.axis_size(axis)
    return lax.ppermute(value, axis, [(i, i ^ distance) for i in range(peers)])


def reduce_scatter_fsdp(term):
    peers = lax.axis_size("fsdp")
    if peers & (peers - 1):
        return lax.psum_scatter(term, "fsdp", scatter_dimension=1, tiled=True)
    index = lax.axis_index("fsdp")
    distance = peers // 2
    while distance >= 1:
        half = term.shape[1] // 2
        keep = (index // distance) % 2
        mine = lax.dynamic_slice_in_dim(term, keep * half, half, 1)
        theirs = lax.dynamic_slice_in_dim(term, (1 - keep) * half, half, 1)
        term = mine + exchange(theirs, "fsdp", distance)
        distance //= 2
    return term


def all_reduce_space(term):
    peers = lax.axis_size("space")
    if peers & (peers - 1):
        return lax.psum(term, "space")
    distance = 1
    while distance < peers:
        term = term + exchange(term, "space", distance)
        distance *= 2
    return term


def local(features, cotangent, tissue, weight):
    edge_cells = features.shape[2]
    channels = weight.shape[2]
    lanes = PAIR * channels
    grid_dims = grid_shape(lax.axis_size("space"))
    index_now = lax.axis_index("space")
    places = (
        index_now // (grid_dims[1] * grid_dims[2]),
        index_now // grid_dims[2] % grid_dims[1],
        index_now % grid_dims[2],
    )
    weight_full = lax.all_gather(weight, "fsdp", axis=1, tiled=True)
    k_fwd = super_kernel(weight_full, channels)
    k_back = jnp.flip(k_fwd, (0, 1, 2)).transpose(0, 1, 2, 4, 3)

    present = tissue[0][:, None, None, None] > 0
    inputs = features[0]
    incoming = cotangent[0]
    masked = jnp.where(present, inputs, jnp.zeros_like(inputs))
    masked_cot = jnp.where(present, incoming, jnp.zeros_like(incoming))

    both = jnp.stack(
        [to_volume(masked, edge_cells, lanes), to_volume(masked_cot, edge_cells, lanes)]
    )
    grown = extend(both, grid_dims, places, (DEPTH, DEPTH, 1))
    grown = jnp.pad(grown, ((0, 0), (0, 0), (0, 0), (1, 1), (0, 0)))
    padded_in = grown[0]

    size_x, size_y, size_s = padded_in.shape[0] - 4, padded_in.shape[1] - 4, padded_in.shape[2] - 4
    k_fwd9 = k_fwd.reshape(3, 3, 3 * lanes, lanes)
    k_back9 = k_back.reshape(3, 3, 3 * lanes, lanes)
    pre_main = tap_dots(z_shift(padded_in, 1, size_s), k_fwd9, size_x + 2, size_y + 2)
    edges_in = jnp.concatenate(
        [z_shift(padded_in, 0, 1), z_shift(padded_in, size_s + 1, 1)], axis=2
    )
    pre_edges = tap_dots(edges_in, k_fwd9, size_x + 2, size_y + 2)
    cot_main = grown[1, 1:-1, 1:-1, 2:-2]
    cot_edges = jnp.concatenate(
        [grown[1, 1:-1, 1:-1, 1:2], grown[1, 1:-1, 1:-1, size_s + 2 : size_s + 3]], axis=2
    )

    def grad_of(pre_part, cot_part):
        gate_part = jax.nn.sigmoid(pre_part)
        slope_part = gate_part * (1.0 + pre_part * (1.0 - gate_part))
        return gate_part, (cot_part.astype(jnp.float32) * slope_part).astype(jnp.bfloat16)

    gate_main, grad_main = grad_of(pre_main, cot_main)
    _, grad_edges = grad_of(pre_edges, cot_edges)

    tissue_mask = tissue[0].astype(jnp.float32)[:, None, None, None]
    pre = to_bricks(pre_main[1:-1, 1:-1], edge_cells, lanes)
    gate_val = to_bricks(gate_main[1:-1, 1:-1], edge_cells, lanes)
    activations = (tissue_mask * (inputs.astype(jnp.float32) + pre * gate_val)).astype(
        jnp.bfloat16
    )

    back_in = jnp.concatenate(
        [
            jnp.concatenate([grad_edges[:, :, :1], grad_main[:, :, :-1]], axis=2),
            grad_main,
            jnp.concatenate([grad_main[:, :, 1:], grad_edges[:, :, 1:]], axis=2),
        ],
        axis=-1,
    )
    back = to_bricks(tap_dots(back_in, k_back9, size_x, size_y), edge_cells, lanes)
    input_grad = (tissue_mask * (incoming.astype(jnp.float32) + back)).astype(jnp.bfloat16)

    total_cells = (
        lax.axis_size("space") * lax.axis_size("fsdp") * BRICK_X * BRICK_Y * BRICK_Z * edge_cells**3
    )
    grad_sup = kernel_grad(padded_in[1:-1, 1:-1, 1:-1], grad_main[1:-1, 1:-1])
    grad_term = fold_kernel_grad(grad_sup, channels) / math.sqrt(total_cells)
    grad_part = reduce_scatter_fsdp(grad_term)
    grad_part = all_reduce_space(grad_part)
    return (activations[None], input_grad[None], grad_part)


def solution(mesh):
    return jax.shard_map(
        local,
        mesh=mesh,
        in_specs=(
            P("fsdp", "space", None, None, None),
            P("fsdp", "space", None, None, None),
            P("fsdp", "space"),
            P(None, "fsdp", None),
        ),
        out_specs=(
            P("fsdp", "space", None, None, None),
            P("fsdp", "space", None, None, None),
            P(None, "fsdp", None),
        ),
        check_vma=False,
    )
```

```python
import math

import jax
import jax.numpy as jnp
from jax import lax
from jax.sharding import PartitionSpec as P

BRICK_X = 2
BRICK_Y = 2
BRICK_Z = 4
PAIR = 2
DEPTH = 2

def from_behind(shard, axis, by):
    peers = lax.axis_size(axis)
    pairs = [(i, i + by) for i in range(peers) if 0 <= i + by < peers]
    return lax.ppermute(shard, axis, pairs)


def grid_shape(number):
    factors = [1, 1, 1]
    places = 0
    while number % 2 == 0:
        factors[places % 3] = factors[places % 3] * 2
        number = number // 2
        places = places + 1
    factors[0] = factors[0] * number
    return factors


def to_volume(bricks, edge_cells, lanes):
    per_brick = edge_cells // PAIR
    blocks = bricks.reshape(
        BRICK_X, BRICK_Y, BRICK_Z, edge_cells, edge_cells, per_brick, lanes
    )
    blocks = blocks.transpose(0, 3, 1, 4, 2, 5, 6)
    return blocks.reshape(
        BRICK_X * edge_cells, BRICK_Y * edge_cells, BRICK_Z * per_brick, lanes
    )


def to_bricks(volume, edge_cells, lanes):
    per_brick = edge_cells // PAIR
    blocks = volume.reshape(
        BRICK_X, edge_cells, BRICK_Y, edge_cells, BRICK_Z, per_brick, lanes
    )
    blocks = blocks.transpose(0, 2, 4, 1, 3, 5, 6)
    return blocks.reshape(
        BRICK_X * BRICK_Y * BRICK_Z, edge_cells, edge_cells, per_brick * lanes
    )


def neighbour_plane(portion, offset, present):
    arrived = from_behind(portion, "space", offset)
    return jnp.where(present, arrived, jnp.zeros_like(arrived))


def extend(volume, grid_dims, places, widths):
    strides = (grid_dims[1] * grid_dims[2], grid_dims[2], 1)
    for axis_pos in range(3):
        axis = axis_pos + 1
        extent = volume.shape[axis]
        width = widths[axis_pos]
        last_layer = lax.slice_in_dim(volume, extent - width, extent, axis=axis)
        first_layer = lax.slice_in_dim(volume, 0, width, axis=axis)
        from_below = neighbour_plane(last_layer, strides[axis_pos], places[axis_pos] > 0)
        from_above = neighbour_plane(
            first_layer, -strides[axis_pos], places[axis_pos] < grid_dims[axis_pos] - 1
        )
        volume = jnp.concatenate([from_below, volume, from_above], axis=axis)
    return volume


def super_kernel(weight_full, channels):
    taps = weight_full.reshape(3, 3, 3, channels, channels)
    zero = jnp.zeros((3, 3, channels, channels), weight_full.dtype)
    rows = []
    for dz in range(3):
        row = []
        for hi in range(PAIR):
            col = []
            for ho in range(PAIR):
                c = 2 * dz - 1 + hi - ho
                col.append(taps[:, :, c] if 0 <= c < 3 else zero)
            row.append(jnp.concatenate(col, axis=-1))
        rows.append(jnp.concatenate(row, axis=-2))
    return jnp.stack(rows, axis=2)


def fold_kernel_grad(grad_sup, channels):
    taps = [None, None, None]
    for dz in range(3):
        for hi in range(PAIR):
            for ho in range(PAIR):
                c = 2 * dz - 1 + hi - ho
                if 0 <= c < 3:
                    block = grad_sup[
                        :, :, dz, hi * channels : (hi + 1) * channels, ho * channels : (ho + 1) * channels
                    ]
                    taps[c] = block if taps[c] is None else taps[c] + block
    return jnp.stack(taps, axis=2).reshape(27, channels, channels)


def z_shift(volume, start, count):
    return jnp.concatenate(
        [volume[:, :, start + dz : start + dz + count] for dz in range(3)], axis=-1
    )


def tap_dots(shifted, kernel, size_x, size_y):
    return lax.conv_general_dilated(
        shifted,
        kernel,
        (1, 1),
        "VALID",
        dimension_numbers=("HWNC", "HWIO", "HWNC"),
        preferred_element_type=jnp.float32,
    )


def kernel_grad(inputs, grads):
    size_x, size_y, size_s, lanes = grads.shape
    shifted = jnp.concatenate([inputs[:, :, dz : dz + size_s] for dz in range(3)], axis=-1)
    rows = grads.reshape(size_x * size_y * size_s, lanes)
    pieces = []
    for a in range(3):
        for b in range(3):
            window = shifted[a : a + size_x, b : b + size_y].reshape(
                size_x * size_y * size_s, 3 * lanes
            )
            pieces.append(
                lax.dot_general(
                    window, rows, (((0,), (0,)), ((), ())), preferred_element_type=jnp.float32
                )
            )
    return jnp.stack(pieces).reshape(3, 3, 3, lanes, lanes)


def exchange(value, axis, distance):
    peers = lax.axis_size(axis)
    return lax.ppermute(value, axis, [(i, i ^ distance) for i in range(peers)])


def reduce_scatter_fsdp(term):
    peers = lax.axis_size("fsdp")
    if peers & (peers - 1):
        return lax.psum_scatter(term, "fsdp", scatter_dimension=1, tiled=True)
    index = lax.axis_index("fsdp")
    distance = peers // 2
    while distance >= 1:
        half = term.shape[1] // 2
        keep = (index // distance) % 2
        mine = lax.dynamic_slice_in_dim(term, keep * half, half, 1)
        theirs = lax.dynamic_slice_in_dim(term, (1 - keep) * half, half, 1)
        term = mine + exchange(theirs, "fsdp", distance)
        distance //= 2
    return term


def all_reduce_space(term):
    peers = lax.axis_size("space")
    if peers & (peers - 1):
        return lax.psum(term, "space")
    distance = 1
    while distance < peers:
        term = term + exchange(term, "space", distance)
        distance *= 2
    return term


def local(features, cotangent, tissue, weight):
    edge_cells = features.shape[2]
    channels = weight.shape[2]
    lanes = PAIR * channels
    grid_dims = grid_shape(lax.axis_size("space"))
    index_now = lax.axis_index("space")
    places = (
        index_now // (grid_dims[1] * grid_dims[2]),
        index_now // grid_dims[2] % grid_dims[1],
        index_now % grid_dims[2],
    )
    weight_full = lax.all_gather(weight, "fsdp", axis=1, tiled=True)
    k_fwd = super_kernel(weight_full, channels)
    k_back = jnp.flip(k_fwd, (0, 1, 2)).transpose(0, 1, 2, 4, 3)

    present = tissue[0][:, None, None, None] > 0
    inputs = features[0]
    incoming = cotangent[0]
    masked = jnp.where(present, inputs, jnp.zeros_like(inputs))
    masked_cot = jnp.where(present, incoming, jnp.zeros_like(incoming))

    both = jnp.stack(
        [to_volume(masked, edge_cells, lanes), to_volume(masked_cot, edge_cells, lanes)]
    )
    grown = extend(both, grid_dims, places, (DEPTH, DEPTH, 1))
    grown = jnp.pad(grown, ((0, 0), (0, 0), (0, 0), (1, 1), (0, 0)))
    padded_in = grown[0]

    size_x, size_y, size_s = padded_in.shape[0] - 4, padded_in.shape[1] - 4, padded_in.shape[2] - 4
    k_fwd9 = k_fwd.reshape(3, 3, 3 * lanes, lanes)
    k_back9 = k_back.reshape(3, 3, 3 * lanes, lanes)
    pre_main = tap_dots(z_shift(padded_in, 1, size_s), k_fwd9, size_x + 2, size_y + 2)
    edges_in = jnp.concatenate(
        [z_shift(padded_in, 0, 1), z_shift(padded_in, size_s + 1, 1)], axis=2
    )
    pre_edges = tap_dots(edges_in, k_fwd9, size_x + 2, size_y + 2)
    cot_main = grown[1, 1:-1, 1:-1, 2:-2]
    cot_edges = jnp.concatenate(
        [grown[1, 1:-1, 1:-1, 1:2], grown[1, 1:-1, 1:-1, size_s + 2 : size_s + 3]], axis=2
    )

    def grad_of(pre_part, cot_part):
        gate_part = jax.nn.sigmoid(pre_part)
        slope_part = gate_part * (1.0 + pre_part * (1.0 - gate_part))
        return gate_part, (cot_part.astype(jnp.float32) * slope_part).astype(jnp.bfloat16)

    gate_main, grad_main = grad_of(pre_main, cot_main)
    _, grad_edges = grad_of(pre_edges, cot_edges)

    tissue_mask = tissue[0].astype(jnp.float32)[:, None, None, None]
    pre = to_bricks(pre_main[1:-1, 1:-1], edge_cells, lanes)
    gate_val = to_bricks(gate_main[1:-1, 1:-1], edge_cells, lanes)
    activations = (tissue_mask * (inputs.astype(jnp.float32) + pre * gate_val)).astype(
        jnp.bfloat16
    )

    total_cells = (
        lax.axis_size("space") * lax.axis_size("fsdp") * BRICK_X * BRICK_Y * BRICK_Z * edge_cells**3
    )
    grad_sup = kernel_grad(padded_in[1:-1, 1:-1, 1:-1], grad_main[1:-1, 1:-1])
    grad_term = fold_kernel_grad(grad_sup, channels) / math.sqrt(total_cells)
    back_in = jnp.concatenate(
        [
            jnp.concatenate([grad_edges[:, :, :1], grad_main[:, :, :-1]], axis=2),
            grad_main,
            jnp.concatenate([grad_main[:, :, 1:], grad_edges[:, :, 1:]], axis=2),
        ],
        axis=-1,
    )
    grad_term, back_in = lax.optimization_barrier((grad_term, back_in))
    back = to_bricks(tap_dots(back_in, k_back9, size_x, size_y), edge_cells, lanes)
    input_grad = (tissue_mask * (incoming.astype(jnp.float32) + back)).astype(jnp.bfloat16)

    grad_part = reduce_scatter_fsdp(grad_term)
    grad_part = all_reduce_space(grad_part)
    return (activations[None], input_grad[None], grad_part)


def solution(mesh):
    return jax.shard_map(
        local,
        mesh=mesh,
        in_specs=(
            P("fsdp", "space", None, None, None),
            P("fsdp", "space", None, None, None),
            P("fsdp", "space"),
            P(None, "fsdp", None),
        ),
        out_specs=(
            P("fsdp", "space", None, None, None),
            P("fsdp", "space", None, None, None),
            P(None, "fsdp", None),
        ),
        check_vma=False,
    )
```

```python
import math

import jax
import jax.numpy as jnp
from jax import lax
from jax.sharding import PartitionSpec as P

BRICK_X = 2
BRICK_Y = 2
BRICK_Z = 4
PAIR = 2
DEPTH = 2

def from_behind(shard, axis, by):
    peers = lax.axis_size(axis)
    pairs = [(i, i + by) for i in range(peers) if 0 <= i + by < peers]
    return lax.ppermute(shard, axis, pairs)


def grid_shape(number):
    factors = [1, 1, 1]
    places = 0
    while number % 2 == 0:
        factors[places % 3] = factors[places % 3] * 2
        number = number // 2
        places = places + 1
    factors[0] = factors[0] * number
    return factors


def to_volume(bricks, edge_cells, lanes):
    per_brick = edge_cells // PAIR
    blocks = bricks.reshape(
        BRICK_X, BRICK_Y, BRICK_Z, edge_cells, edge_cells, per_brick, lanes
    )
    blocks = blocks.transpose(0, 3, 1, 4, 2, 5, 6)
    return blocks.reshape(
        BRICK_X * edge_cells, BRICK_Y * edge_cells, BRICK_Z * per_brick, lanes
    )


def to_bricks(volume, edge_cells, lanes):
    per_brick = edge_cells // PAIR
    blocks = volume.reshape(
        BRICK_X, edge_cells, BRICK_Y, edge_cells, BRICK_Z, per_brick, lanes
    )
    blocks = blocks.transpose(0, 2, 4, 1, 3, 5, 6)
    return blocks.reshape(
        BRICK_X * BRICK_Y * BRICK_Z, edge_cells, edge_cells, per_brick * lanes
    )


def neighbour_plane(portion, offset, present):
    arrived = from_behind(portion, "space", offset)
    return jnp.where(present, arrived, jnp.zeros_like(arrived))


def swap_layers(last_layer, first_layer, stride, size, place, odd_first):
    peers = lax.axis_size("space")
    low = 1 if odd_first else 0
    pairs = []
    for i in range(peers):
        p = (i // stride) % size
        if p % 2 == low and p + 1 < size:
            pairs.append((i, i + stride))
        elif p % 2 != low and p > 0:
            pairs.append((i, i - stride))
    going_up = place % 2 == low
    sent = jnp.where(going_up, last_layer, first_layer)
    return going_up, lax.ppermute(sent, "space", pairs)


def extend(volume, grid_dims, places, widths):
    strides = (grid_dims[1] * grid_dims[2], grid_dims[2], 1)
    for axis_pos in range(3):
        axis = axis_pos + 1
        extent = volume.shape[axis]
        width = widths[axis_pos]
        size = grid_dims[axis_pos]
        place = places[axis_pos]
        last_layer = lax.slice_in_dim(volume, extent - width, extent, axis=axis)
        first_layer = lax.slice_in_dim(volume, 0, width, axis=axis)
        zeros = jnp.zeros_like(last_layer)
        from_below, from_above = zeros, zeros
        for odd_first in ((False, True) if size > 2 else (False,)) if size > 1 else ():
            going_up, arrived = swap_layers(
                last_layer, first_layer, strides[axis_pos], size, place, odd_first
            )
            from_above = jnp.where(going_up & (place < size - 1), arrived, from_above)
            from_below = jnp.where(~going_up & (place > 0), arrived, from_below)
        volume = jnp.concatenate([from_below, volume, from_above], axis=axis)
    return volume


def super_kernel(weight_full, channels):
    taps = weight_full.reshape(3, 3, 3, channels, channels)
    zero = jnp.zeros((3, 3, channels, channels), weight_full.dtype)
    rows = []
    for dz in range(3):
        row = []
        for hi in range(PAIR):
            col = []
            for ho in range(PAIR):
                c = 2 * dz - 1 + hi - ho
                col.append(taps[:, :, c] if 0 <= c < 3 else zero)
            row.append(jnp.concatenate(col, axis=-1))
        rows.append(jnp.concatenate(row, axis=-2))
    return jnp.stack(rows, axis=2)


def fold_kernel_grad(grad_sup, channels):
    taps = [None, None, None]
    for dz in range(3):
        for hi in range(PAIR):
            for ho in range(PAIR):
                c = 2 * dz - 1 + hi - ho
                if 0 <= c < 3:
                    block = grad_sup[
                        :, :, dz, hi * channels : (hi + 1) * channels, ho * channels : (ho + 1) * channels
                    ]
                    taps[c] = block if taps[c] is None else taps[c] + block
    return jnp.stack(taps, axis=2).reshape(27, channels, channels)


def z_shift(volume, start, count):
    return jnp.concatenate(
        [volume[:, :, start + dz : start + dz + count] for dz in range(3)], axis=-1
    )


def tap_dots(shifted, kernel, size_x, size_y):
    return lax.conv_general_dilated(
        shifted,
        kernel,
        (1, 1),
        "VALID",
        dimension_numbers=("HWNC", "HWIO", "HWNC"),
        preferred_element_type=jnp.float32,
    )


def kernel_grad(inputs, grads):
    size_x, size_y, size_s, lanes = grads.shape
    shifted = jnp.concatenate([inputs[:, :, dz : dz + size_s] for dz in range(3)], axis=-1)
    rows = grads.reshape(size_x * size_y * size_s, lanes)
    pieces = []
    for a in range(3):
        for b in range(3):
            window = shifted[a : a + size_x, b : b + size_y].reshape(
                size_x * size_y * size_s, 3 * lanes
            )
            pieces.append(
                lax.dot_general(
                    window, rows, (((0,), (0,)), ((), ())), preferred_element_type=jnp.float32
                )
            )
    return jnp.stack(pieces).reshape(3, 3, 3, lanes, lanes)


def exchange(value, axis, distance):
    peers = lax.axis_size(axis)
    return lax.ppermute(value, axis, [(i, i ^ distance) for i in range(peers)])


def reduce_scatter_fsdp(term):
    peers = lax.axis_size("fsdp")
    if peers & (peers - 1):
        return lax.psum_scatter(term, "fsdp", scatter_dimension=1, tiled=True)
    index = lax.axis_index("fsdp")
    distance = peers // 2
    while distance >= 1:
        half = term.shape[1] // 2
        keep = (index // distance) % 2
        mine = lax.dynamic_slice_in_dim(term, keep * half, half, 1)
        theirs = lax.dynamic_slice_in_dim(term, (1 - keep) * half, half, 1)
        term = mine + exchange(theirs, "fsdp", distance)
        distance //= 2
    return term


def all_reduce_space(term):
    peers = lax.axis_size("space")
    if peers & (peers - 1):
        return lax.psum(term, "space")
    distance = 1
    while distance < peers:
        term = term + exchange(term, "space", distance)
        distance *= 2
    return term


def local(features, cotangent, tissue, weight):
    edge_cells = features.shape[2]
    channels = weight.shape[2]
    lanes = PAIR * channels
    grid_dims = grid_shape(lax.axis_size("space"))
    index_now = lax.axis_index("space")
    places = (
        index_now // (grid_dims[1] * grid_dims[2]),
        index_now // grid_dims[2] % grid_dims[1],
        index_now % grid_dims[2],
    )
    weight_full = lax.all_gather(weight, "fsdp", axis=1, tiled=True)
    k_fwd = super_kernel(weight_full, channels)
    k_back = jnp.flip(k_fwd, (0, 1, 2)).transpose(0, 1, 2, 4, 3)

    present = tissue[0][:, None, None, None] > 0
    inputs = features[0]
    incoming = cotangent[0]
    masked = jnp.where(present, inputs, jnp.zeros_like(inputs))
    masked_cot = jnp.where(present, incoming, jnp.zeros_like(incoming))

    both = jnp.stack(
        [to_volume(masked, edge_cells, lanes), to_volume(masked_cot, edge_cells, lanes)]
    )
    grown = extend(both, grid_dims, places, (DEPTH, DEPTH, 1))
    grown = jnp.pad(grown, ((0, 0), (0, 0), (0, 0), (1, 1), (0, 0)))
    padded_in = grown[0]

    size_x, size_y, size_s = padded_in.shape[0] - 4, padded_in.shape[1] - 4, padded_in.shape[2] - 4
    k_fwd9 = k_fwd.reshape(3, 3, 3 * lanes, lanes)
    k_back9 = k_back.reshape(3, 3, 3 * lanes, lanes)
    pre_main = tap_dots(z_shift(padded_in, 1, size_s), k_fwd9, size_x + 2, size_y + 2)
    edges_in = jnp.concatenate(
        [z_shift(padded_in, 0, 1), z_shift(padded_in, size_s + 1, 1)], axis=2
    )
    pre_edges = tap_dots(edges_in, k_fwd9, size_x + 2, size_y + 2)
    cot_main = grown[1, 1:-1, 1:-1, 2:-2]
    cot_edges = jnp.concatenate(
        [grown[1, 1:-1, 1:-1, 1:2], grown[1, 1:-1, 1:-1, size_s + 2 : size_s + 3]], axis=2
    )

    def grad_of(pre_part, cot_part):
        gate_part = jax.nn.sigmoid(pre_part)
        slope_part = gate_part * (1.0 + pre_part * (1.0 - gate_part))
        return gate_part, (cot_part.astype(jnp.float32) * slope_part).astype(jnp.bfloat16)

    gate_main, grad_main = grad_of(pre_main, cot_main)
    _, grad_edges = grad_of(pre_edges, cot_edges)

    tissue_mask = tissue[0].astype(jnp.float32)[:, None, None, None]
    pre = to_bricks(pre_main[1:-1, 1:-1], edge_cells, lanes)
    gate_val = to_bricks(gate_main[1:-1, 1:-1], edge_cells, lanes)
    activations = (tissue_mask * (inputs.astype(jnp.float32) + pre * gate_val)).astype(
        jnp.bfloat16
    )

    total_cells = (
        lax.axis_size("space") * lax.axis_size("fsdp") * BRICK_X * BRICK_Y * BRICK_Z * edge_cells**3
    )
    grad_sup = kernel_grad(padded_in[1:-1, 1:-1, 1:-1], grad_main[1:-1, 1:-1])
    grad_term = fold_kernel_grad(grad_sup, channels) / math.sqrt(total_cells)
    back_in = jnp.concatenate(
        [
            jnp.concatenate([grad_edges[:, :, :1], grad_main[:, :, :-1]], axis=2),
            grad_main,
            jnp.concatenate([grad_main[:, :, 1:], grad_edges[:, :, 1:]], axis=2),
        ],
        axis=-1,
    )
    grad_term, back_in = lax.optimization_barrier((grad_term, back_in))
    back = to_bricks(tap_dots(back_in, k_back9, size_x, size_y), edge_cells, lanes)
    input_grad = (tissue_mask * (incoming.astype(jnp.float32) + back)).astype(jnp.bfloat16)

    grad_part = reduce_scatter_fsdp(grad_term)
    grad_part = all_reduce_space(grad_part)
    return (activations[None], input_grad[None], grad_part)


def solution(mesh):
    return jax.shard_map(
        local,
        mesh=mesh,
        in_specs=(
            P("fsdp", "space", None, None, None),
            P("fsdp", "space", None, None, None),
            P("fsdp", "space"),
            P(None, "fsdp", None),
        ),
        out_specs=(
            P("fsdp", "space", None, None, None),
            P("fsdp", "space", None, None, None),
            P(None, "fsdp", None),
        ),
        check_vma=False,
    )
```

```python
import math

import jax
import jax.numpy as jnp
from jax import lax
from jax.sharding import PartitionSpec as P

BRICK_X = 2
BRICK_Y = 2
BRICK_Z = 4
PAIR = 2
DEPTH = 2

def from_behind(shard, axis, by):
    peers = lax.axis_size(axis)
    pairs = [(i, i + by) for i in range(peers) if 0 <= i + by < peers]
    return lax.ppermute(shard, axis, pairs)


def grid_shape(number):
    factors = [1, 1, 1]
    places = 0
    while number % 2 == 0:
        factors[places % 3] = factors[places % 3] * 2
        number = number // 2
        places = places + 1
    factors[0] = factors[0] * number
    return factors


def to_volume(bricks, edge_cells, lanes):
    per_brick = edge_cells // PAIR
    blocks = bricks.reshape(
        BRICK_X, BRICK_Y, BRICK_Z, edge_cells, edge_cells, per_brick, lanes
    )
    blocks = blocks.transpose(0, 3, 1, 4, 2, 5, 6)
    return blocks.reshape(
        BRICK_X * edge_cells, BRICK_Y * edge_cells, BRICK_Z * per_brick, lanes
    )


def to_bricks(volume, edge_cells, lanes):
    per_brick = edge_cells // PAIR
    blocks = volume.reshape(
        BRICK_X, edge_cells, BRICK_Y, edge_cells, BRICK_Z, per_brick, lanes
    )
    blocks = blocks.transpose(0, 2, 4, 1, 3, 5, 6)
    return blocks.reshape(
        BRICK_X * BRICK_Y * BRICK_Z, edge_cells, edge_cells, per_brick * lanes
    )


def neighbour_plane(portion, offset, present):
    arrived = from_behind(portion, "space", offset)
    return jnp.where(present, arrived, jnp.zeros_like(arrived))


def swap_layers(last_layer, first_layer, stride, size, place, odd_first):
    peers = lax.axis_size("space")
    low = 1 if odd_first else 0
    pairs = []
    for i in range(peers):
        p = (i // stride) % size
        if p % 2 == low and p + 1 < size:
            pairs.append((i, i + stride))
        elif p % 2 != low and p > 0:
            pairs.append((i, i - stride))
    going_up = place % 2 == low
    sent = jnp.where(going_up, last_layer, first_layer)
    return going_up, lax.ppermute(sent, "space", pairs)


def extend(volume, grid_dims, places, widths):
    strides = (grid_dims[1] * grid_dims[2], grid_dims[2], 1)
    for axis_pos in range(3):
        axis = axis_pos + 1
        extent = volume.shape[axis]
        width = widths[axis_pos]
        size = grid_dims[axis_pos]
        place = places[axis_pos]
        last_layer = lax.slice_in_dim(volume, extent - width, extent, axis=axis)
        first_layer = lax.slice_in_dim(volume, 0, width, axis=axis)
        zeros = jnp.zeros_like(last_layer)
        from_below, from_above = zeros, zeros
        for odd_first in ((False, True) if size > 2 else (False,)) if size > 1 else ():
            going_up, arrived = swap_layers(
                last_layer, first_layer, strides[axis_pos], size, place, odd_first
            )
            from_above = jnp.where(going_up & (place < size - 1), arrived, from_above)
            from_below = jnp.where(~going_up & (place > 0), arrived, from_below)
        volume = jnp.concatenate([from_below, volume, from_above], axis=axis)
    return volume


def super_kernel(weight_full, channels):
    taps = weight_full.reshape(3, 3, 3, channels, channels)
    zero = jnp.zeros((3, 3, channels, channels), weight_full.dtype)
    rows = []
    for dz in range(3):
        row = []
        for hi in range(PAIR):
            col = []
            for ho in range(PAIR):
                c = 2 * dz - 1 + hi - ho
                col.append(taps[:, :, c] if 0 <= c < 3 else zero)
            row.append(jnp.concatenate(col, axis=-1))
        rows.append(jnp.concatenate(row, axis=-2))
    return jnp.stack(rows, axis=2)


def fold_kernel_grad(grad_sup, channels):
    taps = [None, None, None]
    for dz in range(3):
        for hi in range(PAIR):
            for ho in range(PAIR):
                c = 2 * dz - 1 + hi - ho
                if 0 <= c < 3:
                    block = grad_sup[
                        :, :, dz, hi * channels : (hi + 1) * channels, ho * channels : (ho + 1) * channels
                    ]
                    taps[c] = block if taps[c] is None else taps[c] + block
    return jnp.stack(taps, axis=2).reshape(27, channels, channels)


def z_shift(volume, start, count):
    return jnp.concatenate(
        [volume[:, :, start + dz : start + dz + count] for dz in range(3)], axis=-1
    )


def tap_dots(shifted, kernel, size_x, size_y):
    return lax.conv_general_dilated(
        shifted,
        kernel,
        (1, 1),
        "VALID",
        dimension_numbers=("HWNC", "HWIO", "HWNC"),
        preferred_element_type=jnp.float32,
    )


def kernel_grad(inputs, grads):
    size_x, size_y, size_s, lanes = grads.shape
    shifted = jnp.concatenate([inputs[:, :, dz : dz + size_s] for dz in range(3)], axis=-1)
    rows = grads.reshape(size_x * size_y * size_s, lanes)
    pieces = []
    for a in range(3):
        for b in range(3):
            window = shifted[a : a + size_x, b : b + size_y].reshape(
                size_x * size_y * size_s, 3 * lanes
            )
            pieces.append(
                lax.dot_general(
                    window, rows, (((0,), (0,)), ((), ())), preferred_element_type=jnp.float32
                )
            )
    return jnp.stack(pieces).reshape(3, 3, 3, lanes, lanes)


def exchange(value, axis, distance):
    peers = lax.axis_size(axis)
    return lax.ppermute(value, axis, [(i, i ^ distance) for i in range(peers)])


def reduce_scatter_fsdp(term):
    peers = lax.axis_size("fsdp")
    if peers & (peers - 1):
        return lax.psum_scatter(term, "fsdp", scatter_dimension=1, tiled=True)
    index = lax.axis_index("fsdp")
    distance = peers // 2
    while distance >= 1:
        half = term.shape[1] // 2
        keep = (index // distance) % 2
        mine = lax.dynamic_slice_in_dim(term, keep * half, half, 1)
        theirs = lax.dynamic_slice_in_dim(term, (1 - keep) * half, half, 1)
        term = mine + exchange(theirs, "fsdp", distance)
        distance //= 2
    return term


def all_reduce_space(term):
    peers = lax.axis_size("space")
    if peers & (peers - 1):
        return lax.psum(term, "space")
    distance = 1
    while distance < peers:
        term = term + exchange(term, "space", distance)
        distance *= 2
    return term


def local(features, cotangent, tissue, weight):
    edge_cells = features.shape[2]
    channels = weight.shape[2]
    lanes = PAIR * channels
    grid_dims = grid_shape(lax.axis_size("space"))
    index_now = lax.axis_index("space")
    places = (
        index_now // (grid_dims[1] * grid_dims[2]),
        index_now // grid_dims[2] % grid_dims[1],
        index_now % grid_dims[2],
    )
    weight_full = lax.all_gather(weight, "fsdp", axis=1, tiled=True)
    k_fwd = super_kernel(weight_full, channels)
    k_back = jnp.flip(k_fwd, (0, 1, 2)).transpose(0, 1, 2, 4, 3)

    present = tissue[0][:, None, None, None] > 0
    inputs = features[0]
    incoming = cotangent[0]
    masked = jnp.where(present, inputs, jnp.zeros_like(inputs))
    masked_cot = jnp.where(present, incoming, jnp.zeros_like(incoming))

    both = jnp.stack(
        [to_volume(masked, edge_cells, lanes), to_volume(masked_cot, edge_cells, lanes)]
    )
    grown = extend(both, grid_dims, places, (DEPTH, DEPTH, 1))
    grown = jnp.pad(grown, ((0, 0), (0, 0), (0, 0), (1, 1), (0, 0)))
    padded_in = grown[0]

    size_x, size_y, size_s = padded_in.shape[0] - 4, padded_in.shape[1] - 4, padded_in.shape[2] - 4
    k_fwd9 = k_fwd.reshape(3, 3, 3 * lanes, lanes)
    k_back9 = k_back.reshape(3, 3, 3 * lanes, lanes)
    pre_main = tap_dots(z_shift(padded_in, 1, size_s), k_fwd9, size_x + 2, size_y + 2)
    edges_in = jnp.concatenate(
        [z_shift(padded_in, 0, 1), z_shift(padded_in, size_s + 1, 1)], axis=2
    )
    edge_cols = jnp.concatenate(
        [edges_in[a : a + size_x + 2, b : b + size_y + 2] for a in range(3) for b in range(3)],
        axis=-1,
    )
    pre_edges = lax.dot_general(
        edge_cols,
        k_fwd9.reshape(9 * 3 * lanes, lanes),
        (((3,), (0,)), ((), ())),
        preferred_element_type=jnp.float32,
    )
    cot_main = grown[1, 1:-1, 1:-1, 2:-2]
    cot_edges = jnp.concatenate(
        [grown[1, 1:-1, 1:-1, 1:2], grown[1, 1:-1, 1:-1, size_s + 2 : size_s + 3]], axis=2
    )

    def grad_of(pre_part, cot_part):
        gate_part = jax.nn.sigmoid(pre_part)
        slope_part = gate_part * (1.0 + pre_part * (1.0 - gate_part))
        return gate_part, (cot_part.astype(jnp.float32) * slope_part).astype(jnp.bfloat16)

    gate_main, grad_main = grad_of(pre_main, cot_main)
    _, grad_edges = grad_of(pre_edges, cot_edges)

    tissue_mask = tissue[0].astype(jnp.float32)[:, None, None, None]
    pre = to_bricks(pre_main[1:-1, 1:-1], edge_cells, lanes)
    gate_val = to_bricks(gate_main[1:-1, 1:-1], edge_cells, lanes)
    activations = (tissue_mask * (inputs.astype(jnp.float32) + pre * gate_val)).astype(
        jnp.bfloat16
    )

    total_cells = (
        lax.axis_size("space") * lax.axis_size("fsdp") * BRICK_X * BRICK_Y * BRICK_Z * edge_cells**3
    )
    grad_sup = kernel_grad(padded_in[1:-1, 1:-1, 1:-1], grad_main[1:-1, 1:-1])
    grad_term = fold_kernel_grad(grad_sup, channels) / math.sqrt(total_cells)
    grad_term, grad_late = lax.optimization_barrier((grad_term, grad_main))
    back_in = jnp.concatenate(
        [
            jnp.concatenate([grad_edges[:, :, :1], grad_late[:, :, :-1]], axis=2),
            grad_late,
            jnp.concatenate([grad_late[:, :, 1:], grad_edges[:, :, 1:]], axis=2),
        ],
        axis=-1,
    )
    back = to_bricks(tap_dots(back_in, k_back9, size_x, size_y), edge_cells, lanes)
    input_grad = (tissue_mask * (incoming.astype(jnp.float32) + back)).astype(jnp.bfloat16)

    grad_part = reduce_scatter_fsdp(grad_term)
    grad_part = all_reduce_space(grad_part)
    return (activations[None], input_grad[None], grad_part)


def solution(mesh):
    return jax.shard_map(
        local,
        mesh=mesh,
        in_specs=(
            P("fsdp", "space", None, None, None),
            P("fsdp", "space", None, None, None),
            P("fsdp", "space"),
            P(None, "fsdp", None),
        ),
        out_specs=(
            P("fsdp", "space", None, None, None),
            P("fsdp", "space", None, None, None),
            P(None, "fsdp", None),
        ),
        check_vma=False,
    )
```

```python
import math

import jax
import jax.numpy as jnp
from jax import lax
from jax.sharding import PartitionSpec as P

BRICK_X = 2
BRICK_Y = 2
BRICK_Z = 4
PAIR = 2
DEPTH = 2

def from_behind(shard, axis, by):
    peers = lax.axis_size(axis)
    pairs = [(i, i + by) for i in range(peers) if 0 <= i + by < peers]
    return lax.ppermute(shard, axis, pairs)


def grid_shape(number):
    factors = [1, 1, 1]
    places = 0
    while number % 2 == 0:
        factors[places % 3] = factors[places % 3] * 2
        number = number // 2
        places = places + 1
    factors[0] = factors[0] * number
    return factors


def to_volume(bricks, edge_cells, lanes):
    per_brick = edge_cells // PAIR
    blocks = bricks.reshape(
        BRICK_X, BRICK_Y, BRICK_Z, edge_cells, edge_cells, per_brick, lanes
    )
    blocks = blocks.transpose(0, 3, 1, 4, 2, 5, 6)
    return blocks.reshape(
        BRICK_X * edge_cells, BRICK_Y * edge_cells, BRICK_Z * per_brick, lanes
    )


def to_bricks(volume, edge_cells, lanes):
    per_brick = edge_cells // PAIR
    blocks = volume.reshape(
        BRICK_X, edge_cells, BRICK_Y, edge_cells, BRICK_Z, per_brick, lanes
    )
    blocks = blocks.transpose(0, 2, 4, 1, 3, 5, 6)
    return blocks.reshape(
        BRICK_X * BRICK_Y * BRICK_Z, edge_cells, edge_cells, per_brick * lanes
    )


def neighbour_plane(portion, offset, present):
    arrived = from_behind(portion, "space", offset)
    return jnp.where(present, arrived, jnp.zeros_like(arrived))


def swap_layers(last_layer, first_layer, stride, size, place, odd_first):
    peers = lax.axis_size("space")
    low = 1 if odd_first else 0
    pairs = []
    for i in range(peers):
        p = (i // stride) % size
        if p % 2 == low and p + 1 < size:
            pairs.append((i, i + stride))
        elif p % 2 != low and p > 0:
            pairs.append((i, i - stride))
    going_up = place % 2 == low
    sent = jnp.where(going_up, last_layer, first_layer)
    return going_up, lax.ppermute(sent, "space", pairs)


def extend(volume, grid_dims, places, widths):
    strides = (grid_dims[1] * grid_dims[2], grid_dims[2], 1)
    for axis_pos in range(3):
        axis = axis_pos + 1
        extent = volume.shape[axis]
        width = widths[axis_pos]
        size = grid_dims[axis_pos]
        place = places[axis_pos]
        last_layer = lax.slice_in_dim(volume, extent - width, extent, axis=axis)
        first_layer = lax.slice_in_dim(volume, 0, width, axis=axis)
        zeros = jnp.zeros_like(last_layer)
        from_below, from_above = zeros, zeros
        for odd_first in ((False, True) if size > 2 else (False,)) if size > 1 else ():
            going_up, arrived = swap_layers(
                last_layer, first_layer, strides[axis_pos], size, place, odd_first
            )
            from_above = jnp.where(going_up & (place < size - 1), arrived, from_above)
            from_below = jnp.where(~going_up & (place > 0), arrived, from_below)
        volume = jnp.concatenate([from_below, volume, from_above], axis=axis)
    return volume


def super_kernel(weight_full, channels):
    taps = weight_full.reshape(3, 3, 3, channels, channels)
    zero = jnp.zeros((3, 3, channels, channels), weight_full.dtype)
    rows = []
    for dz in range(3):
        row = []
        for hi in range(PAIR):
            col = []
            for ho in range(PAIR):
                c = 2 * dz - 1 + hi - ho
                col.append(taps[:, :, c] if 0 <= c < 3 else zero)
            row.append(jnp.concatenate(col, axis=-1))
        rows.append(jnp.concatenate(row, axis=-2))
    return jnp.stack(rows, axis=2)


def fold_kernel_grad(grad_sup, channels):
    taps = [None, None, None]
    for dz in range(3):
        for hi in range(PAIR):
            for ho in range(PAIR):
                c = 2 * dz - 1 + hi - ho
                if 0 <= c < 3:
                    block = grad_sup[
                        :, :, dz, hi * channels : (hi + 1) * channels, ho * channels : (ho + 1) * channels
                    ]
                    taps[c] = block if taps[c] is None else taps[c] + block
    return jnp.stack(taps, axis=2).reshape(27, channels, channels)


def z_shift(volume, start, count):
    return jnp.concatenate(
        [volume[:, :, start + dz : start + dz + count] for dz in range(3)], axis=-1
    )


def tap_dots(shifted, kernel, size_x, size_y):
    return lax.conv_general_dilated(
        shifted,
        kernel,
        (1, 1),
        "VALID",
        dimension_numbers=("HWNC", "HWIO", "HWNC"),
        preferred_element_type=jnp.float32,
    )


def kernel_grad(inputs, grads):
    size_x, size_y, size_s, lanes = grads.shape
    shifted = jnp.concatenate([inputs[:, :, dz : dz + size_s] for dz in range(3)], axis=-1)
    rows = grads.reshape(size_x * size_y * size_s, lanes)
    pieces = []
    for a in range(3):
        for b in range(3):
            window = shifted[a : a + size_x, b : b + size_y].reshape(
                size_x * size_y * size_s, 3 * lanes
            )
            pieces.append(
                lax.dot_general(
                    window, rows, (((0,), (0,)), ((), ())), preferred_element_type=jnp.float32
                )
            )
    return jnp.stack(pieces).reshape(3, 3, 3, lanes, lanes)


def exchange(value, axis, distance):
    peers = lax.axis_size(axis)
    return lax.ppermute(value, axis, [(i, i ^ distance) for i in range(peers)])


def reduce_scatter_fsdp(term):
    peers = lax.axis_size("fsdp")
    if peers & (peers - 1):
        return lax.psum_scatter(term, "fsdp", scatter_dimension=1, tiled=True)
    index = lax.axis_index("fsdp")
    distance = peers // 2
    while distance >= 1:
        half = term.shape[1] // 2
        keep = (index // distance) % 2
        mine = lax.dynamic_slice_in_dim(term, keep * half, half, 1)
        theirs = lax.dynamic_slice_in_dim(term, (1 - keep) * half, half, 1)
        term = mine + exchange(theirs, "fsdp", distance)
        distance //= 2
    return term


def pairwise_sum(values):
    while len(values) > 1:
        values = [values[m] + values[m + 1] for m in range(0, len(values), 2)]
    return values[0]


def all_reduce_space(term, radix=4):
    peers = lax.axis_size("space")
    if peers & (peers - 1):
        return lax.psum(term, "space")
    distance = 1
    while distance < peers:
        group = min(radix, peers // distance)
        received = [term] + [exchange(term, "space", k * distance) for k in range(1, group)]
        term = pairwise_sum(received)
        distance *= group
    return term


def local(features, cotangent, tissue, weight):
    edge_cells = features.shape[2]
    channels = weight.shape[2]
    lanes = PAIR * channels
    grid_dims = grid_shape(lax.axis_size("space"))
    index_now = lax.axis_index("space")
    places = (
        index_now // (grid_dims[1] * grid_dims[2]),
        index_now // grid_dims[2] % grid_dims[1],
        index_now % grid_dims[2],
    )
    weight_full = lax.all_gather(weight, "fsdp", axis=1, tiled=True)
    k_fwd = super_kernel(weight_full, channels)
    k_back = jnp.flip(k_fwd, (0, 1, 2)).transpose(0, 1, 2, 4, 3)

    present = tissue[0][:, None, None, None] > 0
    inputs = features[0]
    incoming = cotangent[0]
    masked = jnp.where(present, inputs, jnp.zeros_like(inputs))
    masked_cot = jnp.where(present, incoming, jnp.zeros_like(incoming))

    both = jnp.stack(
        [to_volume(masked, edge_cells, lanes), to_volume(masked_cot, edge_cells, lanes)]
    )
    grown = extend(both, grid_dims, places, (DEPTH, DEPTH, 1))
    grown = jnp.pad(grown, ((0, 0), (0, 0), (0, 0), (1, 1), (0, 0)))
    padded_in = grown[0]

    size_x, size_y, size_s = padded_in.shape[0] - 4, padded_in.shape[1] - 4, padded_in.shape[2] - 4
    k_fwd9 = k_fwd.reshape(3, 3, 3 * lanes, lanes)
    k_back9 = k_back.reshape(3, 3, 3 * lanes, lanes)
    pre_main = tap_dots(z_shift(padded_in, 1, size_s), k_fwd9, size_x + 2, size_y + 2)
    edges_in = jnp.concatenate(
        [z_shift(padded_in, 0, 1), z_shift(padded_in, size_s + 1, 1)], axis=2
    )
    edge_cols = jnp.concatenate(
        [edges_in[a : a + size_x + 2, b : b + size_y + 2] for a in range(3) for b in range(3)],
        axis=-1,
    )
    pre_edges = lax.dot_general(
        edge_cols,
        k_fwd9.reshape(9 * 3 * lanes, lanes),
        (((3,), (0,)), ((), ())),
        preferred_element_type=jnp.float32,
    )
    cot_main = grown[1, 1:-1, 1:-1, 2:-2]
    cot_edges = jnp.concatenate(
        [grown[1, 1:-1, 1:-1, 1:2], grown[1, 1:-1, 1:-1, size_s + 2 : size_s + 3]], axis=2
    )

    def grad_of(pre_part, cot_part):
        gate_part = jax.nn.sigmoid(pre_part)
        slope_part = gate_part * (1.0 + pre_part * (1.0 - gate_part))
        return gate_part, (cot_part.astype(jnp.float32) * slope_part).astype(jnp.bfloat16)

    gate_main, grad_main = grad_of(pre_main, cot_main)
    _, grad_edges = grad_of(pre_edges, cot_edges)

    tissue_mask = tissue[0].astype(jnp.float32)[:, None, None, None]
    pre = to_bricks(pre_main[1:-1, 1:-1], edge_cells, lanes)
    gate_val = to_bricks(gate_main[1:-1, 1:-1], edge_cells, lanes)
    activations = (tissue_mask * (inputs.astype(jnp.float32) + pre * gate_val)).astype(
        jnp.bfloat16
    )

    total_cells = (
        lax.axis_size("space") * lax.axis_size("fsdp") * BRICK_X * BRICK_Y * BRICK_Z * edge_cells**3
    )
    grad_sup = kernel_grad(padded_in[1:-1, 1:-1, 1:-1], grad_main[1:-1, 1:-1])
    grad_term = fold_kernel_grad(grad_sup, channels) / math.sqrt(total_cells)
    grad_term, grad_late = lax.optimization_barrier((grad_term, grad_main))
    back_in = jnp.concatenate(
        [
            jnp.concatenate([grad_edges[:, :, :1], grad_late[:, :, :-1]], axis=2),
            grad_late,
            jnp.concatenate([grad_late[:, :, 1:], grad_edges[:, :, 1:]], axis=2),
        ],
        axis=-1,
    )
    back = to_bricks(tap_dots(back_in, k_back9, size_x, size_y), edge_cells, lanes)
    input_grad = (tissue_mask * (incoming.astype(jnp.float32) + back)).astype(jnp.bfloat16)

    grad_part = reduce_scatter_fsdp(grad_term)
    grad_part = all_reduce_space(grad_part)
    return (activations[None], input_grad[None], grad_part)


def solution(mesh):
    return jax.shard_map(
        local,
        mesh=mesh,
        in_specs=(
            P("fsdp", "space", None, None, None),
            P("fsdp", "space", None, None, None),
            P("fsdp", "space"),
            P(None, "fsdp", None),
        ),
        out_specs=(
            P("fsdp", "space", None, None, None),
            P("fsdp", "space", None, None, None),
            P(None, "fsdp", None),
        ),
        check_vma=False,
    )
```

```python
import math

import jax
import jax.numpy as jnp
from jax import lax
from jax.sharding import PartitionSpec as P

BRICK_X = 2
BRICK_Y = 2
BRICK_Z = 4
PAIR = 2
DEPTH = 2

def from_behind(shard, axis, by):
    peers = lax.axis_size(axis)
    pairs = [(i, i + by) for i in range(peers) if 0 <= i + by < peers]
    return lax.ppermute(shard, axis, pairs)


def grid_shape(number):
    factors = [1, 1, 1]
    places = 0
    while number % 2 == 0:
        factors[places % 3] = factors[places % 3] * 2
        number = number // 2
        places = places + 1
    factors[0] = factors[0] * number
    return factors


def to_volume(bricks, edge_cells, lanes):
    per_brick = edge_cells // PAIR
    blocks = bricks.reshape(
        BRICK_X, BRICK_Y, BRICK_Z, edge_cells, edge_cells, per_brick, lanes
    )
    blocks = blocks.transpose(0, 3, 1, 4, 2, 5, 6)
    return blocks.reshape(
        BRICK_X * edge_cells, BRICK_Y * edge_cells, BRICK_Z * per_brick, lanes
    )


def to_bricks(volume, edge_cells, lanes):
    per_brick = edge_cells // PAIR
    blocks = volume.reshape(
        BRICK_X, edge_cells, BRICK_Y, edge_cells, BRICK_Z, per_brick, lanes
    )
    blocks = blocks.transpose(0, 2, 4, 1, 3, 5, 6)
    return blocks.reshape(
        BRICK_X * BRICK_Y * BRICK_Z, edge_cells, edge_cells, per_brick * lanes
    )


def neighbour_plane(portion, offset, present):
    arrived = from_behind(portion, "space", offset)
    return jnp.where(present, arrived, jnp.zeros_like(arrived))


def swap_layers(last_layer, first_layer, stride, size, place, odd_first):
    peers = lax.axis_size("space")
    low = 1 if odd_first else 0
    pairs = []
    for i in range(peers):
        p = (i // stride) % size
        if p % 2 == low and p + 1 < size:
            pairs.append((i, i + stride))
        elif p % 2 != low and p > 0:
            pairs.append((i, i - stride))
    going_up = place % 2 == low
    sent = jnp.where(going_up, last_layer, first_layer)
    return going_up, lax.ppermute(sent, "space", pairs)


def pairing(stride, size, low):
    peers = lax.axis_size("space")
    partner = {}
    for i in range(peers):
        p = (i // stride) % size
        if p % 2 == low and p + 1 < size:
            partner[i] = (i + stride, 1)
        elif p % 2 != low and p > 0:
            partner[i] = (i - stride, -1)
    return partner


def pick(flag, up_value, down_value):
    return jnp.where(flag, up_value, down_value)


def extend_xy(volume, grid_dims, places, width):
    strides = (grid_dims[1] * grid_dims[2], grid_dims[2])
    size_x, size_y = volume.shape[1], volume.shape[2]
    rows = (volume[:, :width], volume[:, size_x - width :])
    cols = (volume[:, :, :width], volume[:, :, size_y - width :])
    corner = [[volume[:, xs, ys] for ys in (slice(0, width), slice(size_y - width, size_y))]
              for xs in (slice(0, width), slice(size_x - width, size_x))]
    lows = [((0, 1) if g > 2 else (0,)) if g > 1 else () for g in grid_dims[:2]]
    inside = [
        (places[axis] > 0, places[axis] < grid_dims[axis] - 1) for axis in range(2)
    ]
    faces = [[jnp.zeros_like(rows[0])] * 2, [jnp.zeros_like(cols[0])] * 2]
    for axis, parts in ((0, rows), (1, cols)):
        for low in lows[axis]:
            pairs = [(i, j) for i, (j, _) in pairing(strides[axis], grid_dims[axis], low).items()]
            up = places[axis] % 2 == low
            arrived = lax.ppermute(pick(up, parts[1], parts[0]), "space", pairs)
            faces[axis][1] = jnp.where(up & inside[axis][1], arrived, faces[axis][1])
            faces[axis][0] = jnp.where(~up & inside[axis][0], arrived, faces[axis][0])
    slots = [[jnp.zeros_like(corner[0][0]) for _ in range(2)] for _ in range(2)]
    for low_x in lows[0]:
        for low_y in lows[1]:
            along_x = pairing(strides[0], grid_dims[0], low_x)
            along_y = pairing(strides[1], grid_dims[1], low_y)
            pairs = [
                (i, i + dx * strides[0] + dy * strides[1])
                for i, (_, dx) in along_x.items()
                if i in along_y
                for dy in (along_y[i][1],)
            ]
            up_x = places[0] % 2 == low_x
            up_y = places[1] % 2 == low_y
            sent = pick(up_x, pick(up_y, corner[1][1], corner[1][0]), pick(up_y, corner[0][1], corner[0][0]))
            arrived = lax.ppermute(sent, "space", pairs)
            for hx in range(2):
                for hy in range(2):
                    here = (up_x == (hx == 1)) & (up_y == (hy == 1)) & inside[0][hx] & inside[1][hy]
                    slots[hx][hy] = jnp.where(here, arrived, slots[hx][hy])
    middle = jnp.concatenate([faces[0][0], volume, faces[0][1]], axis=1)
    low_col = jnp.concatenate([slots[0][0], faces[1][0], slots[1][0]], axis=1)
    high_col = jnp.concatenate([slots[0][1], faces[1][1], slots[1][1]], axis=1)
    return jnp.concatenate([low_col, middle, high_col], axis=2)


def extend(volume, grid_dims, places, widths):
    volume = extend_xy(volume, grid_dims, places, widths[0])
    strides = (grid_dims[1] * grid_dims[2], grid_dims[2], 1)
    for axis_pos in (2,):
        axis = axis_pos + 1
        extent = volume.shape[axis]
        width = widths[axis_pos]
        size = grid_dims[axis_pos]
        place = places[axis_pos]
        last_layer = lax.slice_in_dim(volume, extent - width, extent, axis=axis)
        first_layer = lax.slice_in_dim(volume, 0, width, axis=axis)
        zeros = jnp.zeros_like(last_layer)
        from_below, from_above = zeros, zeros
        for odd_first in ((False, True) if size > 2 else (False,)) if size > 1 else ():
            going_up, arrived = swap_layers(
                last_layer, first_layer, strides[axis_pos], size, place, odd_first
            )
            from_above = jnp.where(going_up & (place < size - 1), arrived, from_above)
            from_below = jnp.where(~going_up & (place > 0), arrived, from_below)
        volume = jnp.concatenate([from_below, volume, from_above], axis=axis)
    return volume


def super_kernel(weight_full, channels):
    taps = weight_full.reshape(3, 3, 3, channels, channels)
    zero = jnp.zeros((3, 3, channels, channels), weight_full.dtype)
    rows = []
    for dz in range(3):
        row = []
        for hi in range(PAIR):
            col = []
            for ho in range(PAIR):
                c = 2 * dz - 1 + hi - ho
                col.append(taps[:, :, c] if 0 <= c < 3 else zero)
            row.append(jnp.concatenate(col, axis=-1))
        rows.append(jnp.concatenate(row, axis=-2))
    return jnp.stack(rows, axis=2)


def fold_kernel_grad(grad_sup, channels):
    taps = [None, None, None]
    for dz in range(3):
        for hi in range(PAIR):
            for ho in range(PAIR):
                c = 2 * dz - 1 + hi - ho
                if 0 <= c < 3:
                    block = grad_sup[
                        :, :, dz, hi * channels : (hi + 1) * channels, ho * channels : (ho + 1) * channels
                    ]
                    taps[c] = block if taps[c] is None else taps[c] + block
    return jnp.stack(taps, axis=2).reshape(27, channels, channels)


def z_shift(volume, start, count):
    return jnp.concatenate(
        [volume[:, :, start + dz : start + dz + count] for dz in range(3)], axis=-1
    )


def tap_dots(shifted, kernel, size_x, size_y):
    return lax.conv_general_dilated(
        shifted,
        kernel,
        (1, 1),
        "VALID",
        dimension_numbers=("HWNC", "HWIO", "HWNC"),
        preferred_element_type=jnp.float32,
    )


def kernel_grad(inputs, grads):
    size_x, size_y, size_s, lanes = grads.shape
    shifted = jnp.concatenate([inputs[:, :, dz : dz + size_s] for dz in range(3)], axis=-1)
    rows = grads.reshape(size_x * size_y * size_s, lanes)
    pieces = []
    for a in range(3):
        for b in range(3):
            window = shifted[a : a + size_x, b : b + size_y].reshape(
                size_x * size_y * size_s, 3 * lanes
            )
            pieces.append(
                lax.dot_general(
                    window, rows, (((0,), (0,)), ((), ())), preferred_element_type=jnp.float32
                )
            )
    return jnp.stack(pieces).reshape(3, 3, 3, lanes, lanes)


def exchange(value, axis, distance):
    peers = lax.axis_size(axis)
    return lax.ppermute(value, axis, [(i, i ^ distance) for i in range(peers)])


def reduce_scatter_fsdp(term):
    peers = lax.axis_size("fsdp")
    if peers & (peers - 1):
        return lax.psum_scatter(term, "fsdp", scatter_dimension=1, tiled=True)
    index = lax.axis_index("fsdp")
    distance = peers // 2
    while distance >= 1:
        half = term.shape[1] // 2
        keep = (index // distance) % 2
        mine = lax.dynamic_slice_in_dim(term, keep * half, half, 1)
        theirs = lax.dynamic_slice_in_dim(term, (1 - keep) * half, half, 1)
        term = mine + exchange(theirs, "fsdp", distance)
        distance //= 2
    return term


def all_reduce_space(term):
    peers = lax.axis_size("space")
    if peers & (peers - 1):
        return lax.psum(term, "space")
    distance = 1
    while distance < peers:
        term = term + exchange(term, "space", distance)
        distance *= 2
    return term


def local(features, cotangent, tissue, weight):
    edge_cells = features.shape[2]
    channels = weight.shape[2]
    lanes = PAIR * channels
    grid_dims = grid_shape(lax.axis_size("space"))
    index_now = lax.axis_index("space")
    places = (
        index_now // (grid_dims[1] * grid_dims[2]),
        index_now // grid_dims[2] % grid_dims[1],
        index_now % grid_dims[2],
    )
    weight_full = lax.all_gather(weight, "fsdp", axis=1, tiled=True)
    k_fwd = super_kernel(weight_full, channels)
    k_back = jnp.flip(k_fwd, (0, 1, 2)).transpose(0, 1, 2, 4, 3)

    present = tissue[0][:, None, None, None] > 0
    inputs = features[0]
    incoming = cotangent[0]
    masked = jnp.where(present, inputs, jnp.zeros_like(inputs))
    masked_cot = jnp.where(present, incoming, jnp.zeros_like(incoming))

    both = jnp.stack(
        [to_volume(masked, edge_cells, lanes), to_volume(masked_cot, edge_cells, lanes)]
    )
    grown = extend(both, grid_dims, places, (DEPTH, DEPTH, 1))
    grown = jnp.pad(grown, ((0, 0), (0, 0), (0, 0), (1, 1), (0, 0)))
    padded_in = grown[0]

    size_x, size_y, size_s = padded_in.shape[0] - 4, padded_in.shape[1] - 4, padded_in.shape[2] - 4
    k_fwd9 = k_fwd.reshape(3, 3, 3 * lanes, lanes)
    k_back9 = k_back.reshape(3, 3, 3 * lanes, lanes)
    pre_main = tap_dots(z_shift(padded_in, 1, size_s), k_fwd9, size_x + 2, size_y + 2)
    edges_in = jnp.concatenate(
        [z_shift(padded_in, 0, 1), z_shift(padded_in, size_s + 1, 1)], axis=2
    )
    edge_cols = jnp.concatenate(
        [edges_in[a : a + size_x + 2, b : b + size_y + 2] for a in range(3) for b in range(3)],
        axis=-1,
    )
    pre_edges = lax.dot_general(
        edge_cols,
        k_fwd9.reshape(9 * 3 * lanes, lanes),
        (((3,), (0,)), ((), ())),
        preferred_element_type=jnp.float32,
    )
    cot_main = grown[1, 1:-1, 1:-1, 2:-2]
    cot_edges = jnp.concatenate(
        [grown[1, 1:-1, 1:-1, 1:2], grown[1, 1:-1, 1:-1, size_s + 2 : size_s + 3]], axis=2
    )

    def grad_of(pre_part, cot_part):
        gate_part = jax.nn.sigmoid(pre_part)
        slope_part = gate_part * (1.0 + pre_part * (1.0 - gate_part))
        return gate_part, (cot_part.astype(jnp.float32) * slope_part).astype(jnp.bfloat16)

    gate_main, grad_main = grad_of(pre_main, cot_main)
    _, grad_edges = grad_of(pre_edges, cot_edges)

    tissue_mask = tissue[0].astype(jnp.float32)[:, None, None, None]
    pre = to_bricks(pre_main[1:-1, 1:-1], edge_cells, lanes)
    gate_val = to_bricks(gate_main[1:-1, 1:-1], edge_cells, lanes)
    activations = (tissue_mask * (inputs.astype(jnp.float32) + pre * gate_val)).astype(
        jnp.bfloat16
    )

    total_cells = (
        lax.axis_size("space") * lax.axis_size("fsdp") * BRICK_X * BRICK_Y * BRICK_Z * edge_cells**3
    )
    grad_sup = kernel_grad(padded_in[1:-1, 1:-1, 1:-1], grad_main[1:-1, 1:-1])
    grad_term = fold_kernel_grad(grad_sup, channels) / math.sqrt(total_cells)
    grad_term, grad_late = lax.optimization_barrier((grad_term, grad_main))
    back_in = jnp.concatenate(
        [
            jnp.concatenate([grad_edges[:, :, :1], grad_late[:, :, :-1]], axis=2),
            grad_late,
            jnp.concatenate([grad_late[:, :, 1:], grad_edges[:, :, 1:]], axis=2),
        ],
        axis=-1,
    )
    back = to_bricks(tap_dots(back_in, k_back9, size_x, size_y), edge_cells, lanes)
    input_grad = (tissue_mask * (incoming.astype(jnp.float32) + back)).astype(jnp.bfloat16)

    grad_part = reduce_scatter_fsdp(grad_term)
    grad_part = all_reduce_space(grad_part)
    return (activations[None], input_grad[None], grad_part)


def solution(mesh):
    return jax.shard_map(
        local,
        mesh=mesh,
        in_specs=(
            P("fsdp", "space", None, None, None),
            P("fsdp", "space", None, None, None),
            P("fsdp", "space"),
            P(None, "fsdp", None),
        ),
        out_specs=(
            P("fsdp", "space", None, None, None),
            P("fsdp", "space", None, None, None),
            P(None, "fsdp", None),
        ),
        check_vma=False,
    )
```

```python
import math

import jax
import jax.numpy as jnp
from jax import lax
from jax.sharding import PartitionSpec as P

BRICK_X = 2
BRICK_Y = 2
BRICK_Z = 4
PAIR = 2
DEPTH = 2

def from_behind(shard, axis, by):
    peers = lax.axis_size(axis)
    pairs = [(i, i + by) for i in range(peers) if 0 <= i + by < peers]
    return lax.ppermute(shard, axis, pairs)


def grid_shape(number):
    factors = [1, 1, 1]
    places = 0
    while number % 2 == 0:
        factors[places % 3] = factors[places % 3] * 2
        number = number // 2
        places = places + 1
    factors[0] = factors[0] * number
    return factors


def to_volume(bricks, edge_cells, lanes):
    per_brick = edge_cells // PAIR
    blocks = bricks.reshape(
        BRICK_X, BRICK_Y, BRICK_Z, edge_cells, edge_cells, per_brick, lanes
    )
    blocks = blocks.transpose(0, 3, 1, 4, 2, 5, 6)
    return blocks.reshape(
        BRICK_X * edge_cells, BRICK_Y * edge_cells, BRICK_Z * per_brick, lanes
    )


def to_bricks(volume, edge_cells, lanes):
    per_brick = edge_cells // PAIR
    blocks = volume.reshape(
        BRICK_X, edge_cells, BRICK_Y, edge_cells, BRICK_Z, per_brick, lanes
    )
    blocks = blocks.transpose(0, 2, 4, 1, 3, 5, 6)
    return blocks.reshape(
        BRICK_X * BRICK_Y * BRICK_Z, edge_cells, edge_cells, per_brick * lanes
    )


def neighbour_plane(portion, offset, present):
    arrived = from_behind(portion, "space", offset)
    return jnp.where(present, arrived, jnp.zeros_like(arrived))


def swap_layers(last_layer, first_layer, stride, size, place, odd_first):
    peers = lax.axis_size("space")
    low = 1 if odd_first else 0
    pairs = []
    for i in range(peers):
        p = (i // stride) % size
        if p % 2 == low and p + 1 < size:
            pairs.append((i, i + stride))
        elif p % 2 != low and p > 0:
            pairs.append((i, i - stride))
    going_up = place % 2 == low
    sent = jnp.where(going_up, last_layer, first_layer)
    return going_up, lax.ppermute(sent, "space", pairs)


def extend(volume, grid_dims, places, widths):
    strides = (grid_dims[1] * grid_dims[2], grid_dims[2], 1)
    for axis_pos in range(3):
        axis = axis_pos + 1
        extent = volume.shape[axis]
        width = widths[axis_pos]
        size = grid_dims[axis_pos]
        place = places[axis_pos]
        last_layer = lax.slice_in_dim(volume, extent - width, extent, axis=axis)
        first_layer = lax.slice_in_dim(volume, 0, width, axis=axis)
        zeros = jnp.zeros_like(last_layer)
        from_below, from_above = zeros, zeros
        for odd_first in ((False, True) if size > 2 else (False,)) if size > 1 else ():
            going_up, arrived = swap_layers(
                last_layer, first_layer, strides[axis_pos], size, place, odd_first
            )
            from_above = jnp.where(going_up & (place < size - 1), arrived, from_above)
            from_below = jnp.where(~going_up & (place > 0), arrived, from_below)
        if axis_pos == 2:
            return volume, from_below, from_above
        volume = jnp.concatenate([from_below, volume, from_above], axis=axis)
    return volume


def super_kernel(weight_full, channels):
    taps = weight_full.reshape(3, 3, 3, channels, channels)
    zero = jnp.zeros((3, 3, channels, channels), weight_full.dtype)
    rows = []
    for dz in range(3):
        row = []
        for hi in range(PAIR):
            col = []
            for ho in range(PAIR):
                c = 2 * dz - 1 + hi - ho
                col.append(taps[:, :, c] if 0 <= c < 3 else zero)
            row.append(jnp.concatenate(col, axis=-1))
        rows.append(jnp.concatenate(row, axis=-2))
    return jnp.stack(rows, axis=2)


def fold_kernel_grad(grad_sup, channels):
    taps = [None, None, None]
    for dz in range(3):
        for hi in range(PAIR):
            for ho in range(PAIR):
                c = 2 * dz - 1 + hi - ho
                if 0 <= c < 3:
                    block = grad_sup[
                        :, :, dz, hi * channels : (hi + 1) * channels, ho * channels : (ho + 1) * channels
                    ]
                    taps[c] = block if taps[c] is None else taps[c] + block
    return jnp.stack(taps, axis=2).reshape(27, channels, channels)


def z_shift(volume, start, count):
    return jnp.concatenate(
        [volume[:, :, start + dz : start + dz + count] for dz in range(3)], axis=-1
    )


def tap_dots(shifted, kernel, size_x, size_y):
    return lax.conv_general_dilated(
        shifted,
        kernel,
        (1, 1),
        "VALID",
        dimension_numbers=("HWNC", "HWIO", "HWNC"),
        preferred_element_type=jnp.float32,
    )


def kernel_grad(shifted, grads):
    size_x, size_y, size_s, lanes = grads.shape
    rows = grads.reshape(size_x * size_y * size_s, lanes)
    pieces = []
    for a in range(3):
        for b in range(3):
            window = shifted[a : a + size_x, b : b + size_y].reshape(
                size_x * size_y * size_s, 3 * lanes
            )
            pieces.append(
                lax.dot_general(
                    window, rows, (((0,), (0,)), ((), ())), preferred_element_type=jnp.float32
                )
            )
    return jnp.stack(pieces).reshape(3, 3, 3, lanes, lanes)


def exchange(value, axis, distance):
    peers = lax.axis_size(axis)
    return lax.ppermute(value, axis, [(i, i ^ distance) for i in range(peers)])


def reduce_scatter_fsdp(term):
    peers = lax.axis_size("fsdp")
    if peers & (peers - 1):
        return lax.psum_scatter(term, "fsdp", scatter_dimension=1, tiled=True)
    index = lax.axis_index("fsdp")
    distance = peers // 2
    while distance >= 1:
        half = term.shape[1] // 2
        keep = (index // distance) % 2
        mine = lax.dynamic_slice_in_dim(term, keep * half, half, 1)
        theirs = lax.dynamic_slice_in_dim(term, (1 - keep) * half, half, 1)
        term = mine + exchange(theirs, "fsdp", distance)
        distance //= 2
    return term


def all_reduce_space(term):
    peers = lax.axis_size("space")
    if peers & (peers - 1):
        return lax.psum(term, "space")
    distance = 1
    while distance < peers:
        term = term + exchange(term, "space", distance)
        distance *= 2
    return term


def local(features, cotangent, tissue, weight):
    edge_cells = features.shape[2]
    channels = weight.shape[2]
    lanes = PAIR * channels
    grid_dims = grid_shape(lax.axis_size("space"))
    index_now = lax.axis_index("space")
    places = (
        index_now // (grid_dims[1] * grid_dims[2]),
        index_now // grid_dims[2] % grid_dims[1],
        index_now % grid_dims[2],
    )
    weight_full = lax.all_gather(weight, "fsdp", axis=1, tiled=True)
    k_fwd = super_kernel(weight_full, channels)
    k_back = jnp.flip(k_fwd, (0, 1, 2)).transpose(0, 1, 2, 4, 3)

    present = tissue[0][:, None, None, None] > 0
    inputs = features[0]
    incoming = cotangent[0]
    masked = jnp.where(present, inputs, jnp.zeros_like(inputs))
    masked_cot = jnp.where(present, incoming, jnp.zeros_like(incoming))

    both = jnp.stack(
        [to_volume(masked, edge_cells, lanes), to_volume(masked_cot, edge_cells, lanes)]
    )
    grown, below, above = extend(both, grid_dims, places, (DEPTH, DEPTH, 1))
    size_x, size_y, size_s = grown.shape[1] - 4, grown.shape[2] - 4, grown.shape[3]
    k_fwd9 = k_fwd.reshape(3, 3, 3 * lanes, lanes)
    k_back9 = k_back.reshape(3, 3, 3 * lanes, lanes)
    padded_in = grown[0]
    shifted_in = jnp.concatenate(
        [
            jnp.concatenate([below[0], padded_in[:, :, :-1]], axis=2),
            padded_in,
            jnp.concatenate([padded_in[:, :, 1:], above[0]], axis=2),
        ],
        axis=-1,
    )
    pre_main = tap_dots(shifted_in, k_fwd9, size_x + 2, size_y + 2)
    zero_plane = jnp.zeros_like(below[0])
    edges_in = jnp.concatenate(
        [
            jnp.concatenate([zero_plane, below[0], padded_in[:, :, :1]], axis=-1),
            jnp.concatenate([padded_in[:, :, -1:], above[0], zero_plane], axis=-1),
        ],
        axis=2,
    )
    edge_cols = jnp.concatenate(
        [edges_in[a : a + size_x + 2, b : b + size_y + 2] for a in range(3) for b in range(3)],
        axis=-1,
    )
    pre_edges = lax.dot_general(
        edge_cols,
        k_fwd9.reshape(9 * 3 * lanes, lanes),
        (((3,), (0,)), ((), ())),
        preferred_element_type=jnp.float32,
    )
    cot_main = grown[1, 1:-1, 1:-1]
    cot_edges = jnp.concatenate([below[1, 1:-1, 1:-1], above[1, 1:-1, 1:-1]], axis=2)

    def grad_of(pre_part, cot_part):
        gate_part = jax.nn.sigmoid(pre_part)
        slope_part = gate_part * (1.0 + pre_part * (1.0 - gate_part))
        return gate_part, (cot_part.astype(jnp.float32) * slope_part).astype(jnp.bfloat16)

    gate_main, grad_main = grad_of(pre_main, cot_main)
    _, grad_edges = grad_of(pre_edges, cot_edges)

    tissue_mask = tissue[0].astype(jnp.float32)[:, None, None, None]
    pre = to_bricks(pre_main[1:-1, 1:-1], edge_cells, lanes)
    gate_val = to_bricks(gate_main[1:-1, 1:-1], edge_cells, lanes)
    activations = (tissue_mask * (inputs.astype(jnp.float32) + pre * gate_val)).astype(
        jnp.bfloat16
    )

    total_cells = (
        lax.axis_size("space") * lax.axis_size("fsdp") * BRICK_X * BRICK_Y * BRICK_Z * edge_cells**3
    )
    grad_sup = kernel_grad(shifted_in[1:-1, 1:-1], grad_main[1:-1, 1:-1])
    grad_term = fold_kernel_grad(grad_sup, channels) / math.sqrt(total_cells)
    grad_term, grad_late = lax.optimization_barrier((grad_term, grad_main))
    back_in = jnp.concatenate(
        [
            jnp.concatenate([grad_edges[:, :, :1], grad_late[:, :, :-1]], axis=2),
            grad_late,
            jnp.concatenate([grad_late[:, :, 1:], grad_edges[:, :, 1:]], axis=2),
        ],
        axis=-1,
    )
    back = to_bricks(tap_dots(back_in, k_back9, size_x, size_y), edge_cells, lanes)
    input_grad = (tissue_mask * (incoming.astype(jnp.float32) + back)).astype(jnp.bfloat16)

    grad_part = reduce_scatter_fsdp(grad_term)
    grad_part = all_reduce_space(grad_part)
    return (activations[None], input_grad[None], grad_part)


def solution(mesh):
    return jax.shard_map(
        local,
        mesh=mesh,
        in_specs=(
            P("fsdp", "space", None, None, None),
            P("fsdp", "space", None, None, None),
            P("fsdp", "space"),
            P(None, "fsdp", None),
        ),
        out_specs=(
            P("fsdp", "space", None, None, None),
            P("fsdp", "space", None, None, None),
            P(None, "fsdp", None),
        ),
        check_vma=False,
    )
```

```python
import math

import jax
import jax.numpy as jnp
from jax import lax
from jax.sharding import PartitionSpec as P

BRICK_X = 2
BRICK_Y = 2
BRICK_Z = 4
PAIR = 2
DEPTH = 2

def from_behind(shard, axis, by):
    peers = lax.axis_size(axis)
    pairs = [(i, i + by) for i in range(peers) if 0 <= i + by < peers]
    return lax.ppermute(shard, axis, pairs)


def grid_shape(number):
    factors = [1, 1, 1]
    places = 0
    while number % 2 == 0:
        factors[places % 3] = factors[places % 3] * 2
        number = number // 2
        places = places + 1
    factors[0] = factors[0] * number
    return factors


def to_volume(bricks, edge_cells, lanes):
    per_brick = edge_cells // PAIR
    blocks = bricks.reshape(
        BRICK_X, BRICK_Y, BRICK_Z, edge_cells, edge_cells, per_brick, lanes
    )
    blocks = blocks.transpose(0, 3, 1, 4, 2, 5, 6)
    return blocks.reshape(
        BRICK_X * edge_cells, BRICK_Y * edge_cells, BRICK_Z * per_brick, lanes
    )


def to_bricks(volume, edge_cells, lanes):
    per_brick = edge_cells // PAIR
    blocks = volume.reshape(
        BRICK_X, edge_cells, BRICK_Y, edge_cells, BRICK_Z, per_brick, lanes
    )
    blocks = blocks.transpose(0, 2, 4, 1, 3, 5, 6)
    return blocks.reshape(
        BRICK_X * BRICK_Y * BRICK_Z, edge_cells, edge_cells, per_brick * lanes
    )


def neighbour_plane(portion, offset, present):
    arrived = from_behind(portion, "space", offset)
    return jnp.where(present, arrived, jnp.zeros_like(arrived))


def swap_layers(last_layer, first_layer, stride, size, place, odd_first):
    peers = lax.axis_size("space")
    low = 1 if odd_first else 0
    pairs = []
    for i in range(peers):
        p = (i // stride) % size
        if p % 2 == low and p + 1 < size:
            pairs.append((i, i + stride))
        elif p % 2 != low and p > 0:
            pairs.append((i, i - stride))
    going_up = place % 2 == low
    sent = jnp.where(going_up, last_layer, first_layer)
    return going_up, lax.ppermute(sent, "space", pairs)


def extend(volume, grid_dims, places, widths):
    strides = (grid_dims[1] * grid_dims[2], grid_dims[2], 1)
    for axis_pos in range(3):
        axis = axis_pos + 1
        extent = volume.shape[axis]
        width = widths[axis_pos]
        size = grid_dims[axis_pos]
        place = places[axis_pos]
        last_layer = lax.slice_in_dim(volume, extent - width, extent, axis=axis)
        first_layer = lax.slice_in_dim(volume, 0, width, axis=axis)
        zeros = jnp.zeros_like(last_layer)
        from_below, from_above = zeros, zeros
        for odd_first in ((False, True) if size > 2 else (False,)) if size > 1 else ():
            going_up, arrived = swap_layers(
                last_layer, first_layer, strides[axis_pos], size, place, odd_first
            )
            from_above = jnp.where(going_up & (place < size - 1), arrived, from_above)
            from_below = jnp.where(~going_up & (place > 0), arrived, from_below)
        if axis_pos == 2:
            return volume, from_below, from_above
        volume = jnp.concatenate([from_below, volume, from_above], axis=axis)
    return volume


def super_kernel(weight_full, channels):
    taps = weight_full.reshape(3, 3, 3, channels, channels)
    zero = jnp.zeros((3, 3, channels, channels), weight_full.dtype)
    rows = []
    for dz in range(3):
        row = []
        for hi in range(PAIR):
            col = []
            for ho in range(PAIR):
                c = 2 * dz - 1 + hi - ho
                col.append(taps[:, :, c] if 0 <= c < 3 else zero)
            row.append(jnp.concatenate(col, axis=-1))
        rows.append(jnp.concatenate(row, axis=-2))
    return jnp.stack(rows, axis=2)


def fold_kernel_grad(grad_sup, channels):
    taps = [None, None, None]
    for dz in range(3):
        for hi in range(PAIR):
            for ho in range(PAIR):
                c = 2 * dz - 1 + hi - ho
                if 0 <= c < 3:
                    block = grad_sup[
                        :, :, dz, hi * channels : (hi + 1) * channels, ho * channels : (ho + 1) * channels
                    ]
                    taps[c] = block if taps[c] is None else taps[c] + block
    return jnp.stack(taps, axis=2).reshape(27, channels, channels)


def z_shift(volume, start, count):
    return jnp.concatenate(
        [volume[:, :, start + dz : start + dz + count] for dz in range(3)], axis=-1
    )


def tap_dots(shifted, kernel, size_x, size_y):
    return lax.conv_general_dilated(
        shifted,
        kernel,
        (1, 1),
        "VALID",
        dimension_numbers=("HWNC", "HWIO", "HWNC"),
        preferred_element_type=jnp.float32,
    )


def kernel_grad(shifted, grads):
    size_x, size_y, size_s, lanes = grads.shape
    rows = grads.reshape(size_x * size_y * size_s, lanes)
    pieces = []
    for a in range(3):
        for b in range(3):
            window = shifted[a : a + size_x, b : b + size_y].reshape(
                size_x * size_y * size_s, 3 * lanes
            )
            pieces.append(
                lax.dot_general(
                    window, rows, (((0,), (0,)), ((), ())), preferred_element_type=jnp.float32
                )
            )
    return jnp.stack(pieces).reshape(3, 3, 3, lanes, lanes)


def exchange(value, axis, distance):
    peers = lax.axis_size(axis)
    return lax.ppermute(value, axis, [(i, i ^ distance) for i in range(peers)])


def reduce_scatter_fsdp(term):
    peers = lax.axis_size("fsdp")
    if peers & (peers - 1):
        return lax.psum_scatter(term, "fsdp", scatter_dimension=1, tiled=True)
    index = lax.axis_index("fsdp")
    distance = peers // 2
    while distance >= 1:
        half = term.shape[1] // 2
        keep = (index // distance) % 2
        mine = lax.dynamic_slice_in_dim(term, keep * half, half, 1)
        theirs = lax.dynamic_slice_in_dim(term, (1 - keep) * half, half, 1)
        term = mine + exchange(theirs, "fsdp", distance)
        distance //= 2
    return term


def pairwise_sum(values):
    while len(values) > 1:
        values = [values[m] + values[m + 1] for m in range(0, len(values), 2)]
    return values[0]


def all_reduce_space(term, radix=4):
    peers = lax.axis_size("space")
    if peers & (peers - 1):
        return lax.psum(term, "space")
    distance = 1
    while distance < peers:
        group = min(radix, peers // distance)
        received = [term] + [exchange(term, "space", k * distance) for k in range(1, group)]
        term = pairwise_sum(received)
        distance *= group
    return term


def local(features, cotangent, tissue, weight):
    edge_cells = features.shape[2]
    channels = weight.shape[2]
    lanes = PAIR * channels
    grid_dims = grid_shape(lax.axis_size("space"))
    index_now = lax.axis_index("space")
    places = (
        index_now // (grid_dims[1] * grid_dims[2]),
        index_now // grid_dims[2] % grid_dims[1],
        index_now % grid_dims[2],
    )
    weight_full = lax.all_gather(weight, "fsdp", axis=1, tiled=True)
    k_fwd = super_kernel(weight_full, channels)
    k_back = jnp.flip(k_fwd, (0, 1, 2)).transpose(0, 1, 2, 4, 3)

    present = tissue[0][:, None, None, None] > 0
    inputs = features[0]
    incoming = cotangent[0]
    masked = jnp.where(present, inputs, jnp.zeros_like(inputs))
    masked_cot = jnp.where(present, incoming, jnp.zeros_like(incoming))

    both = jnp.stack(
        [to_volume(masked, edge_cells, lanes), to_volume(masked_cot, edge_cells, lanes)]
    )
    grown, below, above = extend(both, grid_dims, places, (DEPTH, DEPTH, 1))
    size_x, size_y, size_s = grown.shape[1] - 4, grown.shape[2] - 4, grown.shape[3]
    k_fwd9 = k_fwd.reshape(3, 3, 3 * lanes, lanes)
    k_back9 = k_back.reshape(3, 3, 3 * lanes, lanes)
    padded_in = grown[0]
    shifted_in = jnp.concatenate(
        [
            jnp.concatenate([below[0], padded_in[:, :, :-1]], axis=2),
            padded_in,
            jnp.concatenate([padded_in[:, :, 1:], above[0]], axis=2),
        ],
        axis=-1,
    )
    pre_main = tap_dots(shifted_in, k_fwd9, size_x + 2, size_y + 2)
    zero_plane = jnp.zeros_like(below[0])
    edges_in = jnp.concatenate(
        [
            jnp.concatenate([zero_plane, below[0], padded_in[:, :, :1]], axis=-1),
            jnp.concatenate([padded_in[:, :, -1:], above[0], zero_plane], axis=-1),
        ],
        axis=2,
    )
    edge_cols = jnp.concatenate(
        [edges_in[a : a + size_x + 2, b : b + size_y + 2] for a in range(3) for b in range(3)],
        axis=-1,
    )
    pre_edges = lax.dot_general(
        edge_cols,
        k_fwd9.reshape(9 * 3 * lanes, lanes),
        (((3,), (0,)), ((), ())),
        preferred_element_type=jnp.float32,
    )
    cot_main = grown[1, 1:-1, 1:-1]
    cot_edges = jnp.concatenate([below[1, 1:-1, 1:-1], above[1, 1:-1, 1:-1]], axis=2)

    def grad_of(pre_part, cot_part):
        gate_part = jax.nn.sigmoid(pre_part)
        slope_part = gate_part * (1.0 + pre_part * (1.0 - gate_part))
        return gate_part, (cot_part.astype(jnp.float32) * slope_part).astype(jnp.bfloat16)

    gate_main, grad_main = grad_of(pre_main, cot_main)
    _, grad_edges = grad_of(pre_edges, cot_edges)

    tissue_mask = tissue[0].astype(jnp.float32)[:, None, None, None]
    pre = to_bricks(pre_main[1:-1, 1:-1], edge_cells, lanes)
    gate_val = to_bricks(gate_main[1:-1, 1:-1], edge_cells, lanes)
    activations = (tissue_mask * (inputs.astype(jnp.float32) + pre * gate_val)).astype(
        jnp.bfloat16
    )

    total_cells = (
        lax.axis_size("space") * lax.axis_size("fsdp") * BRICK_X * BRICK_Y * BRICK_Z * edge_cells**3
    )
    grad_sup = kernel_grad(shifted_in[1:-1, 1:-1], grad_main[1:-1, 1:-1])
    grad_term = fold_kernel_grad(grad_sup, channels) / math.sqrt(total_cells)
    grad_term, grad_late = lax.optimization_barrier((grad_term, grad_main))
    grad_part = reduce_scatter_fsdp(grad_term)
    grad_part, grad_late = lax.optimization_barrier((grad_part, grad_late))
    back_in = jnp.concatenate(
        [
            jnp.concatenate([grad_edges[:, :, :1], grad_late[:, :, :-1]], axis=2),
            grad_late,
            jnp.concatenate([grad_late[:, :, 1:], grad_edges[:, :, 1:]], axis=2),
        ],
        axis=-1,
    )
    back = to_bricks(tap_dots(back_in, k_back9, size_x, size_y), edge_cells, lanes)
    input_grad = (tissue_mask * (incoming.astype(jnp.float32) + back)).astype(jnp.bfloat16)

    grad_part = all_reduce_space(grad_part)
    return (activations[None], input_grad[None], grad_part)


def solution(mesh):
    return jax.shard_map(
        local,
        mesh=mesh,
        in_specs=(
            P("fsdp", "space", None, None, None),
            P("fsdp", "space", None, None, None),
            P("fsdp", "space"),
            P(None, "fsdp", None),
        ),
        out_specs=(
            P("fsdp", "space", None, None, None),
            P("fsdp", "space", None, None, None),
            P(None, "fsdp", None),
        ),
        check_vma=False,
    )
```

```python
import math

import jax
import jax.numpy as jnp
from jax import lax
from jax.sharding import PartitionSpec as P

BRICK_X = 2
BRICK_Y = 2
BRICK_Z = 4
PAIR = 2
DEPTH = 2

def from_behind(shard, axis, by):
    peers = lax.axis_size(axis)
    pairs = [(i, i + by) for i in range(peers) if 0 <= i + by < peers]
    return lax.ppermute(shard, axis, pairs)


def grid_shape(number):
    factors = [1, 1, 1]
    places = 0
    while number % 2 == 0:
        factors[places % 3] = factors[places % 3] * 2
        number = number // 2
        places = places + 1
    factors[0] = factors[0] * number
    return factors


def to_volume(bricks, edge_cells, lanes):
    per_brick = edge_cells // PAIR
    blocks = bricks.reshape(
        BRICK_X, BRICK_Y, BRICK_Z, edge_cells, edge_cells, per_brick, lanes
    )
    blocks = blocks.transpose(0, 3, 1, 4, 2, 5, 6)
    return blocks.reshape(
        BRICK_X * edge_cells, BRICK_Y * edge_cells, BRICK_Z * per_brick, lanes
    )


def to_bricks(volume, edge_cells, lanes):
    per_brick = edge_cells // PAIR
    blocks = volume.reshape(
        BRICK_X, edge_cells, BRICK_Y, edge_cells, BRICK_Z, per_brick, lanes
    )
    blocks = blocks.transpose(0, 2, 4, 1, 3, 5, 6)
    return blocks.reshape(
        BRICK_X * BRICK_Y * BRICK_Z, edge_cells, edge_cells, per_brick * lanes
    )


def neighbour_plane(portion, offset, present):
    arrived = from_behind(portion, "space", offset)
    return jnp.where(present, arrived, jnp.zeros_like(arrived))


def swap_layers(last_layer, first_layer, stride, size, place, odd_first):
    peers = lax.axis_size("space")
    low = 1 if odd_first else 0
    pairs = []
    for i in range(peers):
        p = (i // stride) % size
        if p % 2 == low and p + 1 < size:
            pairs.append((i, i + stride))
        elif p % 2 != low and p > 0:
            pairs.append((i, i - stride))
    going_up = place % 2 == low
    sent = jnp.where(going_up, last_layer, first_layer)
    return going_up, lax.ppermute(sent, "space", pairs)


def extend(volume, grid_dims, places, widths):
    strides = (grid_dims[1] * grid_dims[2], grid_dims[2], 1)
    for axis_pos in range(3):
        axis = axis_pos + 1
        extent = volume.shape[axis]
        width = widths[axis_pos]
        size = grid_dims[axis_pos]
        place = places[axis_pos]
        last_layer = lax.slice_in_dim(volume, extent - width, extent, axis=axis)
        first_layer = lax.slice_in_dim(volume, 0, width, axis=axis)
        zeros = jnp.zeros_like(last_layer)
        from_below, from_above = zeros, zeros
        for odd_first in ((False, True) if size > 2 else (False,)) if size > 1 else ():
            going_up, arrived = swap_layers(
                last_layer, first_layer, strides[axis_pos], size, place, odd_first
            )
            from_above = jnp.where(going_up & (place < size - 1), arrived, from_above)
            from_below = jnp.where(~going_up & (place > 0), arrived, from_below)
        if axis_pos == 2:
            return volume, from_below, from_above
        volume = jnp.concatenate([from_below, volume, from_above], axis=axis)
    return volume


def super_kernel(weight_full, channels):
    taps = weight_full.reshape(3, 3, 3, channels, channels)
    zero = jnp.zeros((3, 3, channels, channels), weight_full.dtype)
    rows = []
    for dz in range(3):
        row = []
        for hi in range(PAIR):
            col = []
            for ho in range(PAIR):
                c = 2 * dz - 1 + hi - ho
                col.append(taps[:, :, c] if 0 <= c < 3 else zero)
            row.append(jnp.concatenate(col, axis=-1))
        rows.append(jnp.concatenate(row, axis=-2))
    return jnp.stack(rows, axis=2)


def fold_kernel_grad(grad_sup, channels):
    taps = [None, None, None]
    for dz in range(3):
        for hi in range(PAIR):
            for ho in range(PAIR):
                c = 2 * dz - 1 + hi - ho
                if 0 <= c < 3:
                    block = grad_sup[
                        :, :, dz, hi * channels : (hi + 1) * channels, ho * channels : (ho + 1) * channels
                    ]
                    taps[c] = block if taps[c] is None else taps[c] + block
    return jnp.stack(taps, axis=2).reshape(27, channels, channels)


def z_shift(volume, start, count):
    return jnp.concatenate(
        [volume[:, :, start + dz : start + dz + count] for dz in range(3)], axis=-1
    )


def tap_dots(shifted, kernel, size_x, size_y):
    return lax.conv_general_dilated(
        shifted,
        kernel,
        (1, 1),
        "VALID",
        dimension_numbers=("HWNC", "HWIO", "HWNC"),
        preferred_element_type=jnp.float32,
    )


def kernel_grad(shifted, grads):
    size_x, size_y, size_s, lanes = grads.shape
    rows = grads.reshape(size_x * size_y * size_s, lanes)
    pieces = []
    for a in range(3):
        for b in range(3):
            window = shifted[a : a + size_x, b : b + size_y].reshape(
                size_x * size_y * size_s, 3 * lanes
            )
            pieces.append(
                lax.dot_general(
                    window, rows, (((0,), (0,)), ((), ())), preferred_element_type=jnp.float32
                )
            )
    return jnp.stack(pieces).reshape(3, 3, 3, lanes, lanes)


def exchange(value, axis, distance):
    peers = lax.axis_size(axis)
    return lax.ppermute(value, axis, [(i, i ^ distance) for i in range(peers)])


def reduce_scatter_fsdp(term):
    peers = lax.axis_size("fsdp")
    if peers & (peers - 1):
        return lax.psum_scatter(term, "fsdp", scatter_dimension=1, tiled=True)
    bits = peers.bit_length() - 1
    rows_each = term.shape[1] // peers
    chunks = term.reshape(term.shape[0], *([2] * bits), rows_each, term.shape[2])
    order = (0, *range(bits, 0, -1), bits + 1, bits + 2)
    term = chunks.transpose(order).reshape(term.shape)
    index = lax.axis_index("fsdp")
    distance = 1
    while distance < peers:
        half = term.shape[1] // 2
        keep = (index // distance) % 2
        mine = lax.dynamic_slice_in_dim(term, keep * half, half, 1)
        theirs = lax.dynamic_slice_in_dim(term, (1 - keep) * half, half, 1)
        term = mine + exchange(theirs, "fsdp", distance)
        distance *= 2
    return term


def pairwise_sum(values):
    while len(values) > 1:
        values = [values[m] + values[m + 1] for m in range(0, len(values), 2)]
    return values[0]


def all_reduce_space(term, radix=4):
    peers = lax.axis_size("space")
    if peers & (peers - 1):
        return lax.psum(term, "space")
    distance = 1
    while distance < peers:
        group = min(radix, peers // distance)
        received = [term] + [exchange(term, "space", k * distance) for k in range(1, group)]
        term = pairwise_sum(received)
        distance *= group
    return term


def local(features, cotangent, tissue, weight):
    edge_cells = features.shape[2]
    channels = weight.shape[2]
    lanes = PAIR * channels
    grid_dims = grid_shape(lax.axis_size("space"))
    index_now = lax.axis_index("space")
    places = (
        index_now // (grid_dims[1] * grid_dims[2]),
        index_now // grid_dims[2] % grid_dims[1],
        index_now % grid_dims[2],
    )
    weight_full = lax.all_gather(weight, "fsdp", axis=1, tiled=True)
    k_fwd = super_kernel(weight_full, channels)
    k_back = jnp.flip(k_fwd, (0, 1, 2)).transpose(0, 1, 2, 4, 3)

    present = tissue[0][:, None, None, None] > 0
    inputs = features[0]
    incoming = cotangent[0]
    masked = jnp.where(present, inputs, jnp.zeros_like(inputs))
    masked_cot = jnp.where(present, incoming, jnp.zeros_like(incoming))

    both = jnp.stack(
        [to_volume(masked, edge_cells, lanes), to_volume(masked_cot, edge_cells, lanes)]
    )
    grown, below, above = extend(both, grid_dims, places, (DEPTH, DEPTH, 1))
    size_x, size_y, size_s = grown.shape[1] - 4, grown.shape[2] - 4, grown.shape[3]
    k_fwd9 = k_fwd.reshape(3, 3, 3 * lanes, lanes)
    k_back9 = k_back.reshape(3, 3, 3 * lanes, lanes)
    padded_in = grown[0]
    shifted_in = jnp.concatenate(
        [
            jnp.concatenate([below[0], padded_in[:, :, :-1]], axis=2),
            padded_in,
            jnp.concatenate([padded_in[:, :, 1:], above[0]], axis=2),
        ],
        axis=-1,
    )
    pre_main = tap_dots(shifted_in, k_fwd9, size_x + 2, size_y + 2)
    zero_plane = jnp.zeros_like(below[0])
    edges_in = jnp.concatenate(
        [
            jnp.concatenate([zero_plane, below[0], padded_in[:, :, :1]], axis=-1),
            jnp.concatenate([padded_in[:, :, -1:], above[0], zero_plane], axis=-1),
        ],
        axis=2,
    )
    edge_cols = jnp.concatenate(
        [edges_in[a : a + size_x + 2, b : b + size_y + 2] for a in range(3) for b in range(3)],
        axis=-1,
    )
    pre_edges = lax.dot_general(
        edge_cols,
        k_fwd9.reshape(9 * 3 * lanes, lanes),
        (((3,), (0,)), ((), ())),
        preferred_element_type=jnp.float32,
    )
    cot_main = grown[1, 1:-1, 1:-1]
    cot_edges = jnp.concatenate([below[1, 1:-1, 1:-1], above[1, 1:-1, 1:-1]], axis=2)

    def grad_of(pre_part, cot_part):
        gate_part = jax.nn.sigmoid(pre_part)
        slope_part = gate_part * (1.0 + pre_part * (1.0 - gate_part))
        return gate_part, (cot_part.astype(jnp.float32) * slope_part).astype(jnp.bfloat16)

    gate_main, grad_main = grad_of(pre_main, cot_main)
    _, grad_edges = grad_of(pre_edges, cot_edges)

    tissue_mask = tissue[0].astype(jnp.float32)[:, None, None, None]
    pre = to_bricks(pre_main[1:-1, 1:-1], edge_cells, lanes)
    gate_val = to_bricks(gate_main[1:-1, 1:-1], edge_cells, lanes)
    activations = (tissue_mask * (inputs.astype(jnp.float32) + pre * gate_val)).astype(
        jnp.bfloat16
    )

    total_cells = (
        lax.axis_size("space") * lax.axis_size("fsdp") * BRICK_X * BRICK_Y * BRICK_Z * edge_cells**3
    )
    grad_sup = kernel_grad(shifted_in[1:-1, 1:-1], grad_main[1:-1, 1:-1])
    grad_term = fold_kernel_grad(grad_sup, channels) / math.sqrt(total_cells)
    grad_term, grad_late = lax.optimization_barrier((grad_term, grad_main))
    grad_part = reduce_scatter_fsdp(grad_term)
    grad_part, grad_late = lax.optimization_barrier((grad_part, grad_late))
    back_in = jnp.concatenate(
        [
            jnp.concatenate([grad_edges[:, :, :1], grad_late[:, :, :-1]], axis=2),
            grad_late,
            jnp.concatenate([grad_late[:, :, 1:], grad_edges[:, :, 1:]], axis=2),
        ],
        axis=-1,
    )
    back = to_bricks(tap_dots(back_in, k_back9, size_x, size_y), edge_cells, lanes)
    input_grad = (tissue_mask * (incoming.astype(jnp.float32) + back)).astype(jnp.bfloat16)

    grad_part = all_reduce_space(grad_part)
    return (activations[None], input_grad[None], grad_part)


def solution(mesh):
    return jax.shard_map(
        local,
        mesh=mesh,
        in_specs=(
            P("fsdp", "space", None, None, None),
            P("fsdp", "space", None, None, None),
            P("fsdp", "space"),
            P(None, "fsdp", None),
        ),
        out_specs=(
            P("fsdp", "space", None, None, None),
            P("fsdp", "space", None, None, None),
            P(None, "fsdp", None),
        ),
        check_vma=False,
    )
```

```python
import math

import jax
import jax.numpy as jnp
from jax import lax
from jax.sharding import PartitionSpec as P

BRICK_X = 2
BRICK_Y = 2
BRICK_Z = 4
PAIR = 2
DEPTH = 2


def from_behind(shard, axis, by):
    peers = lax.axis_size(axis)
    pairs = [(i, i + by) for i in range(peers) if 0 <= i + by < peers]
    return lax.ppermute(shard, axis, pairs)


def grid_shape(number):
    factors = [1, 1, 1]
    places = 0
    while number % 2 == 0:
        factors[places % 3] = factors[places % 3] * 2
        number = number // 2
        places = places + 1
    factors[0] = factors[0] * number
    return factors


def to_volume(bricks, edge_cells, lanes):
    per_brick = edge_cells // PAIR
    blocks = bricks.reshape(
        BRICK_X, BRICK_Y, BRICK_Z, edge_cells, edge_cells, per_brick, lanes
    )
    blocks = blocks.transpose(0, 3, 1, 4, 2, 5, 6)
    return blocks.reshape(
        BRICK_X * edge_cells, BRICK_Y * edge_cells, BRICK_Z * per_brick, lanes
    )


def to_bricks(volume, edge_cells, lanes):
    per_brick = edge_cells // PAIR
    blocks = volume.reshape(
        BRICK_X, edge_cells, BRICK_Y, edge_cells, BRICK_Z, per_brick, lanes
    )
    blocks = blocks.transpose(0, 2, 4, 1, 3, 5, 6)
    return blocks.reshape(
        BRICK_X * BRICK_Y * BRICK_Z, edge_cells, edge_cells, per_brick * lanes
    )


def neighbour_plane(portion, offset, present):
    arrived = from_behind(portion, "space", offset)
    return jnp.where(present, arrived, jnp.zeros_like(arrived))


def swap_layers(last_layer, first_layer, stride, size, place, odd_first):
    peers = lax.axis_size("space")
    low = 1 if odd_first else 0
    pairs = []
    for i in range(peers):
        p = (i // stride) % size
        if p % 2 == low and p + 1 < size:
            pairs.append((i, i + stride))
        elif p % 2 != low and p > 0:
            pairs.append((i, i - stride))
    going_up = place % 2 == low
    sent = jnp.where(going_up, last_layer, first_layer)
    return going_up, lax.ppermute(sent, "space", pairs)


def extend(volume, grid_dims, places, widths):
    strides = (grid_dims[1] * grid_dims[2], grid_dims[2], 1)
    for axis_pos in range(3):
        axis = axis_pos + 1
        extent = volume.shape[axis]
        width = widths[axis_pos]
        size = grid_dims[axis_pos]
        place = places[axis_pos]
        last_layer = lax.slice_in_dim(volume, extent - width, extent, axis=axis)
        first_layer = lax.slice_in_dim(volume, 0, width, axis=axis)
        zeros = jnp.zeros_like(last_layer)
        from_below, from_above = zeros, zeros
        for odd_first in ((False, True) if size > 2 else (False,)) if size > 1 else ():
            going_up, arrived = swap_layers(
                last_layer, first_layer, strides[axis_pos], size, place, odd_first
            )
            from_above = jnp.where(going_up & (place < size - 1), arrived, from_above)
            from_below = jnp.where(~going_up & (place > 0), arrived, from_below)
        if axis_pos == 2:
            return volume, from_below, from_above
        volume = jnp.concatenate([from_below, volume, from_above], axis=axis)
    return volume


def super_kernel(weight_full, channels):
    taps = weight_full.reshape(3, 3, 3, channels, channels)
    zero = jnp.zeros((3, 3, channels, channels), weight_full.dtype)
    rows = []
    for dz in range(3):
        row = []
        for hi in range(PAIR):
            col = []
            for ho in range(PAIR):
                c = 2 * dz - 1 + hi - ho
                col.append(taps[:, :, c] if 0 <= c < 3 else zero)
            row.append(jnp.concatenate(col, axis=-1))
        rows.append(jnp.concatenate(row, axis=-2))
    return jnp.stack(rows, axis=2)


def fold_kernel_grad(grad_sup, channels):
    taps = [None, None, None]
    for dz in range(3):
        for hi in range(PAIR):
            for ho in range(PAIR):
                c = 2 * dz - 1 + hi - ho
                if 0 <= c < 3:
                    block = grad_sup[
                        :, :, dz, hi * channels : (hi + 1) * channels, ho * channels : (ho + 1) * channels
                    ]
                    taps[c] = block if taps[c] is None else taps[c] + block
    return jnp.stack(taps, axis=2).reshape(27, channels, channels)


def z_shift(volume, start, count):
    return jnp.concatenate(
        [volume[:, :, start + dz : start + dz + count] for dz in range(3)], axis=-1
    )


def tap_dots(shifted, kernel, size_x, size_y):
    return lax.conv_general_dilated(
        shifted,
        kernel,
        (1, 1),
        "VALID",
        dimension_numbers=("HWNC", "HWIO", "HWNC"),
        preferred_element_type=jnp.float32,
    )


def kernel_grad(shifted, grads):
    size_x, size_y, size_s, lanes = grads.shape
    rows = grads.reshape(size_x * size_y * size_s, lanes)
    pieces = []
    for a in range(3):
        for b in range(3):
            window = shifted[a : a + size_x, b : b + size_y].reshape(
                size_x * size_y * size_s, 3 * lanes
            )
            pieces.append(
                lax.dot_general(
                    window, rows, (((0,), (0,)), ((), ())), preferred_element_type=jnp.float32
                )
            )
    return jnp.stack(pieces).reshape(3, 3, 3, lanes, lanes)


def exchange(value, axis, distance):
    peers = lax.axis_size(axis)
    return lax.ppermute(value, axis, [(i, i ^ distance) for i in range(peers)])


def reduce_scatter_fsdp(term):
    peers = lax.axis_size("fsdp")
    if peers & (peers - 1):
        return lax.psum_scatter(term, "fsdp", scatter_dimension=1, tiled=True)
    bits = peers.bit_length() - 1
    rows_each = term.shape[1] // peers
    chunks = term.reshape(term.shape[0], *([2] * bits), rows_each, term.shape[2])
    order = (0, *range(bits, 0, -1), bits + 1, bits + 2)
    term = chunks.transpose(order).reshape(term.shape)
    index = lax.axis_index("fsdp")
    distance = 1
    while distance < peers:
        half = term.shape[1] // 2
        keep = (index // distance) % 2
        mine = lax.dynamic_slice_in_dim(term, keep * half, half, 1)
        theirs = lax.dynamic_slice_in_dim(term, (1 - keep) * half, half, 1)
        term = mine + exchange(theirs, "fsdp", distance)
        distance *= 2
    return term


def pairwise_sum(values):
    while len(values) > 1:
        values = [values[m] + values[m + 1] for m in range(0, len(values), 2)]
    return values[0]


def all_reduce_space(term, radix=8):
    peers = lax.axis_size("space")
    if peers & (peers - 1):
        return lax.psum(term, "space")
    distance = 1
    while distance < peers:
        group = min(radix, peers // distance)
        received = [term] + [exchange(term, "space", k * distance) for k in range(1, group)]
        term = pairwise_sum(received)
        distance *= group
    return term


def local(features, cotangent, tissue, weight):
    edge_cells = features.shape[2]
    channels = weight.shape[2]
    lanes = PAIR * channels
    grid_dims = grid_shape(lax.axis_size("space"))
    index_now = lax.axis_index("space")
    places = (
        index_now // (grid_dims[1] * grid_dims[2]),
        index_now // grid_dims[2] % grid_dims[1],
        index_now % grid_dims[2],
    )
    weight_full = lax.all_gather(weight, "fsdp", axis=1, tiled=True)
    k_fwd = super_kernel(weight_full, channels)
    k_back = jnp.flip(k_fwd, (0, 1, 2)).transpose(0, 1, 2, 4, 3)

    present = tissue[0][:, None, None, None] > 0
    inputs = features[0]
    incoming = cotangent[0]
    masked = jnp.where(present, inputs, jnp.zeros_like(inputs))
    masked_cot = jnp.where(present, incoming, jnp.zeros_like(incoming))

    both = jnp.stack(
        [to_volume(masked, edge_cells, lanes), to_volume(masked_cot, edge_cells, lanes)]
    )
    grown, below, above = extend(both, grid_dims, places, (DEPTH, DEPTH, 1))
    size_x, size_y, size_s = grown.shape[1] - 4, grown.shape[2] - 4, grown.shape[3]
    k_fwd9 = k_fwd.reshape(3, 3, 3 * lanes, lanes)
    k_back9 = k_back.reshape(3, 3, 3 * lanes, lanes)
    padded_in = grown[0]
    shifted_in = jnp.concatenate(
        [
            jnp.concatenate([below[0], padded_in[:, :, :-1]], axis=2),
            padded_in,
            jnp.concatenate([padded_in[:, :, 1:], above[0]], axis=2),
        ],
        axis=-1,
    )
    pre_main = tap_dots(shifted_in, k_fwd9, size_x + 2, size_y + 2)
    zero_plane = jnp.zeros_like(below[0])
    edges_in = jnp.concatenate(
        [
            jnp.concatenate([zero_plane, below[0], padded_in[:, :, :1]], axis=-1),
            jnp.concatenate([padded_in[:, :, -1:], above[0], zero_plane], axis=-1),
        ],
        axis=2,
    )
    edge_cols = jnp.concatenate(
        [edges_in[a : a + size_x + 2, b : b + size_y + 2] for a in range(3) for b in range(3)],
        axis=-1,
    )
    pre_edges = lax.dot_general(
        edge_cols,
        k_fwd9.reshape(9 * 3 * lanes, lanes),
        (((3,), (0,)), ((), ())),
        preferred_element_type=jnp.float32,
    )
    cot_main = grown[1, 1:-1, 1:-1]
    cot_edges = jnp.concatenate([below[1, 1:-1, 1:-1], above[1, 1:-1, 1:-1]], axis=2)

    def grad_of(pre_part, cot_part):
        gate_part = jax.nn.sigmoid(pre_part)
        slope_part = gate_part * (1.0 + pre_part * (1.0 - gate_part))
        return gate_part, (cot_part.astype(jnp.float32) * slope_part).astype(jnp.bfloat16)

    gate_main, grad_main = grad_of(pre_main, cot_main)
    _, grad_edges = grad_of(pre_edges, cot_edges)

    tissue_mask = tissue[0].astype(jnp.float32)[:, None, None, None]
    pre = to_bricks(pre_main[1:-1, 1:-1], edge_cells, lanes)
    gate_val = to_bricks(gate_main[1:-1, 1:-1], edge_cells, lanes)
    activations = (tissue_mask * (inputs.astype(jnp.float32) + pre * gate_val)).astype(
        jnp.bfloat16
    )

    total_cells = (
        lax.axis_size("space") * lax.axis_size("fsdp") * BRICK_X * BRICK_Y * BRICK_Z * edge_cells**3
    )
    grad_sup = kernel_grad(shifted_in[1:-1, 1:-1], grad_main[1:-1, 1:-1])
    grad_term = fold_kernel_grad(grad_sup, channels) / math.sqrt(total_cells)
    grad_term, grad_late = lax.optimization_barrier((grad_term, grad_main))
    grad_part = reduce_scatter_fsdp(grad_term)
    grad_part, grad_late = lax.optimization_barrier((grad_part, grad_late))
    back_in = jnp.concatenate(
        [
            jnp.concatenate([grad_edges[:, :, :1], grad_late[:, :, :-1]], axis=2),
            grad_late,
            jnp.concatenate([grad_late[:, :, 1:], grad_edges[:, :, 1:]], axis=2),
        ],
        axis=-1,
    )
    back = to_bricks(tap_dots(back_in, k_back9, size_x, size_y), edge_cells, lanes)
    input_grad = (tissue_mask * (incoming.astype(jnp.float32) + back)).astype(jnp.bfloat16)

    grad_part = all_reduce_space(grad_part)
    return (activations[None], input_grad[None], grad_part)


def solution(mesh):
    return jax.shard_map(
        local,
        mesh=mesh,
        in_specs=(
            P("fsdp", "space", None, None, None),
            P("fsdp", "space", None, None, None),
            P("fsdp", "space"),
            P(None, "fsdp", None),
        ),
        out_specs=(
            P("fsdp", "space", None, None, None),
            P("fsdp", "space", None, None, None),
            P(None, "fsdp", None),
        ),
        check_vma=False,
    )
```

```python
import math

import jax
import jax.numpy as jnp
from jax import lax
from jax.sharding import PartitionSpec as P

BRICK_X = 2
BRICK_Y = 2
BRICK_Z = 4
PAIR = 2
DEPTH = 2

def from_behind(shard, axis, by):
    peers = lax.axis_size(axis)
    pairs = [(i, i + by) for i in range(peers) if 0 <= i + by < peers]
    return lax.ppermute(shard, axis, pairs)


def grid_shape(number):
    factors = [1, 1, 1]
    places = 0
    while number % 2 == 0:
        factors[places % 3] = factors[places % 3] * 2
        number = number // 2
        places = places + 1
    factors[0] = factors[0] * number
    return factors


def to_volume(bricks, edge_cells, lanes):
    per_brick = edge_cells // PAIR
    blocks = bricks.reshape(
        BRICK_X, BRICK_Y, BRICK_Z, edge_cells, edge_cells, per_brick, lanes
    )
    blocks = blocks.transpose(0, 3, 1, 4, 2, 5, 6)
    return blocks.reshape(
        BRICK_X * edge_cells, BRICK_Y * edge_cells, BRICK_Z * per_brick, lanes
    )


def to_bricks(volume, edge_cells, lanes):
    per_brick = edge_cells // PAIR
    blocks = volume.reshape(
        BRICK_X, edge_cells, BRICK_Y, edge_cells, BRICK_Z, per_brick, lanes
    )
    blocks = blocks.transpose(0, 2, 4, 1, 3, 5, 6)
    return blocks.reshape(
        BRICK_X * BRICK_Y * BRICK_Z, edge_cells, edge_cells, per_brick * lanes
    )


def neighbour_plane(portion, offset, present):
    arrived = from_behind(portion, "space", offset)
    return jnp.where(present, arrived, jnp.zeros_like(arrived))


def swap_layers(last_layer, first_layer, stride, size, place, odd_first):
    peers = lax.axis_size("space")
    low = 1 if odd_first else 0
    pairs = []
    for i in range(peers):
        p = (i // stride) % size
        if p % 2 == low and p + 1 < size:
            pairs.append((i, i + stride))
        elif p % 2 != low and p > 0:
            pairs.append((i, i - stride))
    going_up = place % 2 == low
    sent = jnp.where(going_up, last_layer, first_layer)
    return going_up, lax.ppermute(sent, "space", pairs)


def extend(volume, grid_dims, places, widths):
    strides = (grid_dims[1] * grid_dims[2], grid_dims[2], 1)
    for axis_pos in range(3):
        axis = axis_pos + 1
        extent = volume.shape[axis]
        width = widths[axis_pos]
        size = grid_dims[axis_pos]
        place = places[axis_pos]
        last_layer = lax.slice_in_dim(volume, extent - width, extent, axis=axis)
        first_layer = lax.slice_in_dim(volume, 0, width, axis=axis)
        zeros = jnp.zeros_like(last_layer)
        from_below, from_above = zeros, zeros
        for odd_first in ((False, True) if size > 2 else (False,)) if size > 1 else ():
            going_up, arrived = swap_layers(
                last_layer, first_layer, strides[axis_pos], size, place, odd_first
            )
            from_above = jnp.where(going_up & (place < size - 1), arrived, from_above)
            from_below = jnp.where(~going_up & (place > 0), arrived, from_below)
        if axis_pos == 2:
            return volume, from_below, from_above
        volume = jnp.concatenate([from_below, volume, from_above], axis=axis)
    return volume


def super_kernel(weight_full, channels):
    taps = weight_full.reshape(3, 3, 3, channels, channels)
    zero = jnp.zeros((3, 3, channels, channels), weight_full.dtype)
    rows = []
    for dz in range(3):
        row = []
        for hi in range(PAIR):
            col = []
            for ho in range(PAIR):
                c = 2 * dz - 1 + hi - ho
                col.append(taps[:, :, c] if 0 <= c < 3 else zero)
            row.append(jnp.concatenate(col, axis=-1))
        rows.append(jnp.concatenate(row, axis=-2))
    return jnp.stack(rows, axis=2)


def fold_kernel_grad(grad_sup, channels):
    taps = [None, None, None]
    for dz in range(3):
        for hi in range(PAIR):
            for ho in range(PAIR):
                c = 2 * dz - 1 + hi - ho
                if 0 <= c < 3:
                    block = grad_sup[
                        :, :, dz, hi * channels : (hi + 1) * channels, ho * channels : (ho + 1) * channels
                    ]
                    taps[c] = block if taps[c] is None else taps[c] + block
    return jnp.stack(taps, axis=2).reshape(27, channels, channels)


def z_shift(volume, start, count):
    return jnp.concatenate(
        [volume[:, :, start + dz : start + dz + count] for dz in range(3)], axis=-1
    )


def tap_dots(shifted, kernel, size_x, size_y):
    return lax.conv_general_dilated(
        shifted,
        kernel,
        (1, 1),
        "VALID",
        dimension_numbers=("HWNC", "HWIO", "HWNC"),
        preferred_element_type=jnp.float32,
    )


def kernel_grad(shifted, grads):
    size_x, size_y, size_s, lanes = grads.shape
    rows = grads.reshape(size_x * size_y * size_s, lanes)
    pieces = []
    for a in range(3):
        for b in range(3):
            window = shifted[a : a + size_x, b : b + size_y].reshape(
                size_x * size_y * size_s, 3 * lanes
            )
            pieces.append(
                lax.dot_general(
                    window, rows, (((0,), (0,)), ((), ())), preferred_element_type=jnp.float32
                )
            )
    return jnp.stack(pieces).reshape(3, 3, 3, lanes, lanes)


def exchange(value, axis, distance):
    peers = lax.axis_size(axis)
    return lax.ppermute(value, axis, [(i, i ^ distance) for i in range(peers)])


def reduce_scatter_fsdp(term):
    peers = lax.axis_size("fsdp")
    if peers & (peers - 1):
        return lax.psum_scatter(term, "fsdp", scatter_dimension=1, tiled=True)
    bits = peers.bit_length() - 1
    rows_each = term.shape[1] // peers
    chunks = term.reshape(term.shape[0], *([2] * bits), rows_each, term.shape[2])
    order = (0, *range(bits, 0, -1), bits + 1, bits + 2)
    term = chunks.transpose(order).reshape(term.shape)
    index = lax.axis_index("fsdp")
    distance = 1
    while distance < peers:
        half = term.shape[1] // 2
        keep = (index // distance) % 2
        mine = lax.dynamic_slice_in_dim(term, keep * half, half, 1)
        theirs = lax.dynamic_slice_in_dim(term, (1 - keep) * half, half, 1)
        term = mine + exchange(theirs, "fsdp", distance)
        distance *= 2
    return term


def pairwise_sum(values):
    while len(values) > 1:
        values = [values[m] + values[m + 1] for m in range(0, len(values), 2)]
    return values[0]


def all_reduce_space(term, radix=4):
    peers = lax.axis_size("space")
    if peers & (peers - 1):
        return lax.psum(term, "space")
    bits = peers.bit_length() - 1
    per_round = radix.bit_length() - 1
    groups = [list(range(b, min(b + per_round, bits))) for b in range(1, bits, per_round)]
    groups = groups + ([[0]] if bits > 0 else [])
    for group in groups:
        received = [term]
        for c in range(1, 1 << len(group)):
            distance = sum(1 << bit for j, bit in enumerate(group) if (c >> j) & 1)
            received.append(exchange(term, "space", distance))
        term = pairwise_sum(received)
    return term


def local(features, cotangent, tissue, weight):
    edge_cells = features.shape[2]
    channels = weight.shape[2]
    lanes = PAIR * channels
    grid_dims = grid_shape(lax.axis_size("space"))
    index_now = lax.axis_index("space")
    places = (
        index_now // (grid_dims[1] * grid_dims[2]),
        index_now // grid_dims[2] % grid_dims[1],
        index_now % grid_dims[2],
    )
    weight_full = lax.all_gather(weight, "fsdp", axis=1, tiled=True)
    k_fwd = super_kernel(weight_full, channels)
    k_back = jnp.flip(k_fwd, (0, 1, 2)).transpose(0, 1, 2, 4, 3)

    present = tissue[0][:, None, None, None] > 0
    inputs = features[0]
    incoming = cotangent[0]
    masked = jnp.where(present, inputs, jnp.zeros_like(inputs))
    masked_cot = jnp.where(present, incoming, jnp.zeros_like(incoming))

    both = jnp.stack(
        [to_volume(masked, edge_cells, lanes), to_volume(masked_cot, edge_cells, lanes)]
    )
    grown, below, above = extend(both, grid_dims, places, (DEPTH, DEPTH, 1))
    size_x, size_y, size_s = grown.shape[1] - 4, grown.shape[2] - 4, grown.shape[3]
    k_fwd9 = k_fwd.reshape(3, 3, 3 * lanes, lanes)
    k_back9 = k_back.reshape(3, 3, 3 * lanes, lanes)
    padded_in = grown[0]
    shifted_in = jnp.concatenate(
        [
            jnp.concatenate([below[0], padded_in[:, :, :-1]], axis=2),
            padded_in,
            jnp.concatenate([padded_in[:, :, 1:], above[0]], axis=2),
        ],
        axis=-1,
    )
    pre_main = tap_dots(shifted_in, k_fwd9, size_x + 2, size_y + 2)
    zero_plane = jnp.zeros_like(below[0])
    edges_in = jnp.concatenate(
        [
            jnp.concatenate([zero_plane, below[0], padded_in[:, :, :1]], axis=-1),
            jnp.concatenate([padded_in[:, :, -1:], above[0], zero_plane], axis=-1),
        ],
        axis=2,
    )
    edge_cols = jnp.concatenate(
        [edges_in[a : a + size_x + 2, b : b + size_y + 2] for a in range(3) for b in range(3)],
        axis=-1,
    )
    pre_edges = lax.dot_general(
        edge_cols,
        k_fwd9.reshape(9 * 3 * lanes, lanes),
        (((3,), (0,)), ((), ())),
        preferred_element_type=jnp.float32,
    )
    cot_main = grown[1, 1:-1, 1:-1]
    cot_edges = jnp.concatenate([below[1, 1:-1, 1:-1], above[1, 1:-1, 1:-1]], axis=2)

    def grad_of(pre_part, cot_part):
        gate_part = jax.nn.sigmoid(pre_part)
        slope_part = gate_part * (1.0 + pre_part * (1.0 - gate_part))
        return gate_part, (cot_part.astype(jnp.float32) * slope_part).astype(jnp.bfloat16)

    gate_main, grad_main = grad_of(pre_main, cot_main)
    _, grad_edges = grad_of(pre_edges, cot_edges)

    tissue_mask = tissue[0].astype(jnp.float32)[:, None, None, None]
    pre = to_bricks(pre_main[1:-1, 1:-1], edge_cells, lanes)
    gate_val = to_bricks(gate_main[1:-1, 1:-1], edge_cells, lanes)
    activations = (tissue_mask * (inputs.astype(jnp.float32) + pre * gate_val)).astype(
        jnp.bfloat16
    )

    total_cells = (
        lax.axis_size("space") * lax.axis_size("fsdp") * BRICK_X * BRICK_Y * BRICK_Z * edge_cells**3
    )
    grad_sup = kernel_grad(shifted_in[1:-1, 1:-1], grad_main[1:-1, 1:-1])
    grad_term = fold_kernel_grad(grad_sup, channels) / math.sqrt(total_cells)
    grad_term, grad_late = lax.optimization_barrier((grad_term, grad_main))
    grad_part = reduce_scatter_fsdp(grad_term)
    grad_part, grad_late = lax.optimization_barrier((grad_part, grad_late))
    back_in = jnp.concatenate(
        [
            jnp.concatenate([grad_edges[:, :, :1], grad_late[:, :, :-1]], axis=2),
            grad_late,
            jnp.concatenate([grad_late[:, :, 1:], grad_edges[:, :, 1:]], axis=2),
        ],
        axis=-1,
    )
    back = to_bricks(tap_dots(back_in, k_back9, size_x, size_y), edge_cells, lanes)
    input_grad = (tissue_mask * (incoming.astype(jnp.float32) + back)).astype(jnp.bfloat16)

    grad_part = all_reduce_space(grad_part)
    return (activations[None], input_grad[None], grad_part)


def solution(mesh):
    return jax.shard_map(
        local,
        mesh=mesh,
        in_specs=(
            P("fsdp", "space", None, None, None),
            P("fsdp", "space", None, None, None),
            P("fsdp", "space"),
            P(None, "fsdp", None),
        ),
        out_specs=(
            P("fsdp", "space", None, None, None),
            P("fsdp", "space", None, None, None),
            P(None, "fsdp", None),
        ),
        check_vma=False,
    )
```
